128 devices in a mesh: ang: 4 (over x), slab: 32 (over z, y, core).
Axes of the slice: x: 4, y: 4, z: 4, core: 2. Of those that a mesh axis runs over, the one named last changes fastest.
Arguments:
- projections: bfloat16 [64, 1024, 2048], P('slab', 'ang'), may hold values from -6 to 6
- dest_plane: int32 [64, 1024], P('slab'), may hold values from 0 to 1023, as said below
- sub_offset: int32 [64, 1024], P('slab'), may hold values from 0 to 7, as said below
- ky_bin: int32 [64, 1024], P('slab'), may hold values from 0 to 7, as said below
Outputs:
- volume_real: float32 [1024, 8, 2048], P('slab', None, 'ang')
- volume_imag: float32 [1024, 8, 2048], P('slab', None, 'ang')
The draws below stay inside these ranges and needn't reach their ends.
Inputs may be any that keep to these rules, and one draw needn't show every extreme that they name: With f = q for q < 512 and q - 1024 otherwise, and an integer s of 8 to 16 for each projection, e = floor(64 * 1024 f / (1024 * s)) and dest_plane = floor(e / 8) + 512. Among the 2 projections of one slab index at most 128 rows fall on one aligned block of 32 planes; some slab index reaches 128. sub_offset = e mod 8 for the e of dest_plane. With f as for dest_plane and an integer r of 1 to 8 for each projection, ky_bin = floor((f + 512) r / 1024).
All inputs are finite; a program needn't handle non-finite values.
Results may differ from the reference program's by a relative error of at most 0.0085.
Values may be sent and summed in bfloat16 or wider, within the bound.
No kernel may reach another device: no remote copies, remote signals or barrier semaphores. Data moves between devices by JAX's collectives and lax.ppermute only.
A program may use at most 192 MiB of HBM per device.

```python
import math
import jax
import jax.numpy as jnp
from jax import lax

W = 2048
H = 1024
PROJ_DEV = 2
KY = 8
REG_ITERS = 2
NPROJ = 64
NZ = 1024


def cone_choice(key):
    chosen = jax.random.randint(jax.random.fold_in(key, 12), (), 0, NPROJ // PROJ_DEV)
    widest = (chosen * PROJ_DEV + PROJ_DEV + jax.random.randint(jax.random.fold_in(key, 13), (), 0, NPROJ - PROJ_DEV)) % NPROJ
    return (chosen, widest)


def row_frequency():
    row_index = jnp.arange(H, dtype=jnp.int32)
    return jnp.where(row_index < H // 2, row_index, row_index - H)


def cone_layout(key):
    slopes = jax.random.randint(jax.random.fold_in(key, 11), (NPROJ,), 8, 17)
    chosen, widest = cone_choice(key)
    proj_index = jnp.arange(NPROJ, dtype=jnp.int32)
    slopes = jnp.where(proj_index // PROJ_DEV == chosen, 16, slopes)
    slopes = jnp.where(proj_index == widest, 8, slopes)
    frequency = row_frequency()
    eighths = frequency[None, :] * (64 * NZ) // (H * slopes[:, None])
    return ((eighths // 8 + NZ // 2).astype(jnp.int32), (eighths % 8).astype(jnp.int32))


def draw_dest_plane(key, part):
    return cone_layout(key)[0]


def draw_sub_offset(key, part):
    return cone_layout(key)[1]


def draw_ky_bin(key, part):
    rates = jax.random.randint(jax.random.fold_in(key, 21), (NPROJ,), 1, KY + 1)
    chosen, widest = cone_choice(key)
    proj_index = jnp.arange(NPROJ, dtype=jnp.int32)
    rates = jnp.where(proj_index == widest, KY, rates)
    frequency = row_frequency()
    return ((frequency[None, :] + H // 2) * rates[:, None] // H).astype(jnp.int32)


def block_scale(own_key, extent, cuts, smallest, largest):
    gain, own = 1.0, jax.random.fold_in(own_key, 6)
    for position, shards_of in cuts:
        steps = jnp.exp(jax.random.uniform(jax.random.fold_in(own, position), (shards_of,), jnp.float32, smallest / len(cuts), largest / len(cuts)))
        gain = gain * jnp.repeat(steps, extent[position] // shards_of).reshape([-1 if axis == position else 1 for axis in range(len(extent))])
    return gain


def centred(rng, shape, spread, bound, shards=(), kind=jnp.bfloat16):
    entries = jax.random.normal(rng, shape, jnp.float32) * spread
    if len(shards) > 0:
        entries = block_scale(rng, shape, shards, -0.22, 0.18) * entries
    return jnp.clip(entries, min=-bound, max=bound).astype(kind)


def setup_inputs(seed: int = 0) -> dict:
    arg_keys = jax.random.split(jax.random.key(seed), 5)
    projections = centred(arg_keys[0], (NPROJ, H, W), 1.0, 6.0, ((0, 32), (1, 4)))
    dest_plane = draw_dest_plane(jax.random.fold_in(arg_keys[4], 71), 0)
    sub_offset = draw_sub_offset(jax.random.fold_in(arg_keys[4], 71), 0)
    ky_bin = draw_ky_bin(jax.random.fold_in(arg_keys[4], 71), 0)
    return dict(projections=projections, dest_plane=dest_plane, sub_offset=sub_offset, ky_bin=ky_bin)


def trig_tables(length):
    row_index = jnp.arange(length, dtype=jnp.int32)[:, None]
    column = jnp.arange(length, dtype=jnp.int32)[None, :]
    phase_angle = (row_index * column % length).astype(jnp.float32) * (2.0 * math.pi / length)
    return (jnp.cos(phase_angle).astype(jnp.bfloat16), jnp.sin(phase_angle).astype(jnp.bfloat16))

def grid_rows(buffer, centre, eighth, ky_index, rows, density):
    for shift in range(-2, 4):
        distance = shift - eighth.astype(jnp.float32) * 0.125
        weight = (jnp.exp(-0.5 * distance * distance) * density).astype(jnp.bfloat16)
        weight = lax.optimization_barrier(weight).astype(jnp.float32)
        index = (centre + (shift + 3)) * KY + ky_index
        buffer = buffer.at[index].add(weight[:, None] * rows)
    return buffer

def reference(projections, dest_plane, sub_offset, ky_bin):
    cosines_w, sines_w = trig_tables(W)
    table = jnp.concatenate([cosines_w, sines_w], axis=1)
    cosines_h, sines_h = trig_tables(H)
    unitary = 1.0 / math.sqrt(H * W)
    density = 1.0 / math.sqrt(NPROJ)

    def accumulate(volume, scan_item):
        projection_image, centre, eighth, ky_index = scan_item
        transformed = jnp.dot(projection_image, table, preferred_element_type=jnp.float32)
        row_spectra = jnp.concatenate([transformed[:, :W], -transformed[:, W:]], axis=1).astype(jnp.bfloat16)
        cosine_part = jnp.dot(cosines_h, row_spectra, preferred_element_type=jnp.float32)
        sine_part = jnp.dot(sines_h, row_spectra, preferred_element_type=jnp.float32)
        real_part = cosine_part[:, :W] + sine_part[:, W:]
        imag_part = cosine_part[:, W:] - sine_part[:, :W]
        spectral_rows = (jnp.concatenate([real_part, imag_part], axis=1) * unitary).astype(jnp.bfloat16)
        return (grid_rows(volume, centre, eighth, ky_index, spectral_rows, density), None)
    volume, unused = lax.scan(accumulate, jnp.zeros(((NZ + 6) * KY, 2 * W), jnp.float32), (projections, dest_plane, sub_offset, ky_bin))
    gridded = volume.reshape(NZ + 6, KY, 2 * W)[3:-3]
    iterate = gridded
    for sweep in range(REG_ITERS):
        bordered = jnp.pad(iterate, ((1, 1), (0, 0), (0, 0)))
        iterate = iterate - 0.25 * (iterate - gridded + (2.0 * iterate - bordered[:-2] - bordered[2:]))
    return (iterate[:, :, :W], iterate[:, :, W:])
```

```python
import math

import jax
import jax.numpy as jnp
from jax import lax
from jax.sharding import PartitionSpec as P

KY = 8
NZ = 1024
REG_ITERS = 2
SPREAD_LOW = 2
SPREAD_HIGH = 3
HALO = SPREAD_LOW + SPREAD_HIGH


def phase_parts(rows, cols, length):
    row_index = jnp.arange(rows, dtype=jnp.int32)[:, None]
    column = cols[None, :]
    phase_angle = (row_index * column % length).astype(jnp.float32) * (2.0 * math.pi / length)
    return jnp.cos(phase_angle), jnp.sin(phase_angle)


def trig_tables(length):
    split = 1 << (int(math.log2(length)) // 2)
    cos_hi, sin_hi = phase_parts(length, jnp.arange(length // split, dtype=jnp.int32) * split, length)
    cos_lo, sin_lo = phase_parts(length, jnp.arange(split, dtype=jnp.int32), length)
    cosine = cos_hi[:, :, None] * cos_lo[:, None, :] - sin_hi[:, :, None] * sin_lo[:, None, :]
    sine = sin_hi[:, :, None] * cos_lo[:, None, :] + cos_hi[:, :, None] * sin_lo[:, None, :]
    return cosine.reshape(length, length), sine.reshape(length, length)


def on_device(projections, dest_plane, sub_offset, ky_bin):
    count_ang = lax.axis_size("ang")
    count_slab = lax.axis_size("slab")
    local_count, quarter, full_width = projections.shape
    height = quarter * count_ang
    cols = full_width // count_ang
    nz = NZ
    z_dev = nz // count_slab

    cosines_w, sines_w = trig_tables(full_width)
    table = jnp.stack(
        [cosines_w.reshape(full_width, count_ang, cols), -sines_w.reshape(full_width, count_ang, cols)],
        axis=2,
    ).astype(jnp.bfloat16)
    transformed = jnp.einsum(
        "rw,wdcx->drcx",
        projections.reshape(local_count * quarter, full_width),
        table,
        preferred_element_type=jnp.float32,
    ).astype(jnp.bfloat16)
    exchanged = lax.all_to_all(transformed, "ang", split_axis=0, concat_axis=0, tiled=True)
    exchanged = exchanged.reshape(count_ang, local_count, quarter, 2, cols)
    real_in = exchanged[:, :, :, 0]
    imag_in = exchanged[:, :, :, 1]
    rhs = jnp.stack(
        [jnp.stack([real_in, imag_in], axis=3), jnp.stack([imag_in, -real_in], axis=3)], axis=0
    )
    cosines_h, sines_h = trig_tables(height)
    lhs = jnp.stack([cosines_h, sines_h], axis=1).astype(jnp.bfloat16)
    lhs = lhs.reshape(height, 2, count_ang, quarter)
    unitary = 1.0 / math.sqrt(height * full_width)
    spectrum = jnp.einsum("qcsh,csphdx->pqdx", lhs, rhs, preferred_element_type=jnp.float32)
    spectrum = (spectrum * unitary).astype(jnp.bfloat16)
    total_cols = 2 * cols
    spectral_rows = spectrum.reshape(local_count * height, total_cols)

    per_proj = 2 * z_dev
    capacity = local_count * per_proj
    edges = jnp.arange(count_slab + 1, dtype=jnp.int32) * z_dev
    start = jnp.sum(
        (dest_plane[:, None, :] < edges[None, :, None]).astype(jnp.int32), axis=2
    )
    counts = start[:, 1:] - start[:, :-1]
    slot = jnp.arange(per_proj, dtype=jnp.int32)
    forder = start[:, :-1, None] + slot[None, None, :]
    valid = slot[None, None, :] < counts[:, :, None]
    row_q = (forder + height // 2) % height
    source = jnp.where(valid, row_q + jnp.arange(local_count, dtype=jnp.int32)[:, None, None] * height, 0)
    source = jnp.transpose(source, (1, 0, 2)).reshape(-1)
    valid = jnp.transpose(valid, (1, 0, 2)).reshape(-1)
    outgoing = jnp.where(valid[:, None], spectral_rows[source], jnp.zeros((), jnp.bfloat16))
    block_of = jnp.repeat(jnp.arange(count_slab, dtype=jnp.int32), capacity)
    flat_plane = dest_plane.reshape(-1)[source]
    flat_eighth = sub_offset.reshape(-1)[source]
    flat_ky = ky_bin.reshape(-1)[source]
    labels = jnp.where(
        valid, ((flat_plane - block_of * z_dev) * 8 + flat_eighth) * KY + flat_ky, -1
    )
    arrived = lax.all_to_all(
        outgoing.reshape(count_slab, capacity, total_cols), "slab", split_axis=0, concat_axis=0, tiled=True
    ).reshape(-1, total_cols)
    arrived_tags = lax.all_to_all(
        labels.reshape(count_slab, capacity), "slab", split_axis=0, concat_axis=0, tiled=True
    ).reshape(-1)

    tag_ok = arrived_tags >= 0
    tag = jnp.maximum(arrived_tags, 0)
    arrived_ky = tag % KY
    arrived_eighth = tag // KY % 8
    arrived_plane = tag // (8 * KY)
    density = 1.0 / math.sqrt(local_count * count_slab)
    slots = z_dev + HALO + 1
    dest_index = jnp.arange(slots * KY, dtype=jnp.int32)[:, None]
    weights = jnp.zeros((slots * KY, arrived.shape[0]), jnp.bfloat16)
    for shift in range(-SPREAD_LOW, SPREAD_HIGH + 1):
        distance = shift - arrived_eighth.astype(jnp.float32) * 0.125
        weight = (jnp.exp(-0.5 * distance * distance) * density).astype(jnp.bfloat16)
        index = (arrived_plane + (shift + SPREAD_HIGH)) * KY + arrived_ky
        hit = (dest_index == index[None, :]) & tag_ok[None, :]
        weights = jnp.where(hit, weight[None, :], weights)
    padded = jnp.dot(weights, arrived, preferred_element_type=jnp.float32)
    padded = padded.reshape(slots, KY, total_cols)

    me = lax.axis_index("slab")
    forward = [(i, i + 1) for i in range(count_slab - 1)]
    backward = [(i + 1, i) for i in range(count_slab - 1)]
    from_lower = lax.ppermute(padded[slots - HALO:], "slab", forward)
    from_upper = lax.ppermute(padded[:HALO], "slab", backward)
    window = padded[1:slots - 1]
    wide = z_dev + 2 * REG_ITERS
    gridded = window.at[:HALO].add(from_lower).at[wide - HALO:].add(from_upper)
    plane_global = me * z_dev + jnp.arange(wide, dtype=jnp.int32) - REG_ITERS
    inside = ((plane_global >= 0) & (plane_global < nz))[:, None, None]
    gridded = jnp.where(inside, gridded, 0.0)
    iterate = gridded
    for sweep in range(REG_ITERS):
        centre = iterate[1:-1]
        target = gridded[sweep + 1:wide - sweep - 1]
        iterate = centre - 0.25 * (
            centre - target + (2.0 * centre - iterate[:-2] - iterate[2:])
        )
        iterate = jnp.where(inside[sweep + 1:wide - sweep - 1], iterate, 0.0)
    return (iterate[:, :, :cols], iterate[:, :, cols:])


def solution(mesh):
    placed = (P("slab", "ang", None), P("slab", None), P("slab", None), P("slab", None))
    return jax.shard_map(
        on_device,
        mesh=mesh,
        in_specs=placed,
        out_specs=(P("slab", None, "ang"), P("slab", None, "ang")),
        check_vma=False,
    )
```

```python
import math

import jax
import jax.numpy as jnp
from jax import lax
from jax.sharding import PartitionSpec as P

KY = 8
NZ = 1024
REG_ITERS = 2
SPREAD_LOW = 2
SPREAD_HIGH = 3
HALO = SPREAD_LOW + SPREAD_HIGH


def phase_parts(rows, cols, length):
    row_index = jnp.arange(rows, dtype=jnp.int32)[:, None]
    column = cols[None, :]
    phase_angle = (row_index * column % length).astype(jnp.float32) * (2.0 * math.pi / length)
    return jnp.cos(phase_angle), jnp.sin(phase_angle)


def trig_tables(length):
    split = 1 << (int(math.log2(length)) // 2)
    cos_hi, sin_hi = phase_parts(length, jnp.arange(length // split, dtype=jnp.int32) * split, length)
    cos_lo, sin_lo = phase_parts(length, jnp.arange(split, dtype=jnp.int32), length)
    cosine = cos_hi[:, :, None] * cos_lo[:, None, :] - sin_hi[:, :, None] * sin_lo[:, None, :]
    sine = sin_hi[:, :, None] * cos_lo[:, None, :] + cos_hi[:, :, None] * sin_lo[:, None, :]
    return cosine.reshape(length, length), sine.reshape(length, length)


def on_device(projections, dest_plane, sub_offset, ky_bin):
    count_ang = lax.axis_size("ang")
    count_slab = lax.axis_size("slab")
    local_count, quarter, full_width = projections.shape
    height = quarter * count_ang
    cols = full_width // count_ang
    total_cols = 2 * cols
    nz = NZ
    z_dev = nz // count_slab
    per_proj = 2 * z_dev

    cosines_w, sines_w = trig_tables(full_width)
    table = jnp.stack(
        [cosines_w.reshape(full_width, count_ang, cols), -sines_w.reshape(full_width, count_ang, cols)],
        axis=2,
    ).astype(jnp.bfloat16).reshape(full_width, count_ang * total_cols)
    cosines_h, sines_h = trig_tables(height)
    lhs = jnp.concatenate([cosines_h, sines_h], axis=1).astype(jnp.bfloat16)
    unitary = 1.0 / math.sqrt(height * full_width)

    edges = jnp.arange(count_slab + 1, dtype=jnp.int32) * z_dev
    start = jnp.sum((dest_plane[:, None, :] < edges[None, :, None]).astype(jnp.int32), axis=2)
    counts = start[:, 1:] - start[:, :-1]
    slot = jnp.arange(per_proj, dtype=jnp.int32)
    valid = slot[None, None, :] < counts[:, :, None]
    row_q = (start[:, :-1, None] + slot[None, None, :] + height // 2) % height
    q_iota = jnp.arange(height, dtype=jnp.int32)
    select = ((row_q[..., None] == q_iota) & valid[..., None]).astype(jnp.bfloat16)
    label_cols = jnp.stack(
        [dest_plane % z_dev, sub_offset, ky_bin, jnp.ones_like(ky_bin)], axis=-1
    ).astype(jnp.bfloat16)
    labels = jnp.einsum("pbjq,pqk->bpjk", select, label_cols, preferred_element_type=jnp.float32)
    arrived_labels = lax.all_to_all(labels, "slab", split_axis=0, concat_axis=0, tiled=True)

    arrived_rows = []
    for p in range(local_count):
        transformed = jnp.dot(projections[p], table, preferred_element_type=jnp.float32)
        transformed = transformed.astype(jnp.bfloat16).reshape(quarter, count_ang, total_cols)
        transformed = jnp.transpose(transformed, (1, 0, 2))
        received = lax.all_to_all(transformed, "ang", split_axis=0, concat_axis=0, tiled=True)
        received = received.reshape(height, total_cols)
        swapped = jnp.concatenate([received[:, cols:], -received[:, :cols]], axis=1)
        rhs = jnp.concatenate([received, swapped], axis=0)
        spectrum = jnp.dot(lhs, rhs, preferred_element_type=jnp.float32)
        spectrum = (spectrum * unitary).astype(jnp.bfloat16)
        packed = jnp.einsum("bjq,qc->bjc", select[p], spectrum, preferred_element_type=jnp.bfloat16)
        arrived_rows.append(
            lax.all_to_all(packed, "slab", split_axis=0, concat_axis=0, tiled=True).reshape(-1, total_cols)
        )

    density = 1.0 / math.sqrt(local_count * count_slab)
    slots = z_dev + HALO + 1
    dest_index = jnp.arange(slots * KY, dtype=jnp.int32)[:, None]
    padded = jnp.zeros((slots * KY, total_cols), jnp.float32)
    for p in range(local_count):
        tags = arrived_labels[:, p].reshape(-1, 4)
        arrived_plane = tags[:, 0].astype(jnp.int32)
        arrived_eighth = tags[:, 1].astype(jnp.int32)
        arrived_ky = tags[:, 2].astype(jnp.int32)
        tag_ok = tags[:, 3] > 0.5
        weights = jnp.zeros((slots * KY, tags.shape[0]), jnp.bfloat16)
        for shift in range(-SPREAD_LOW, SPREAD_HIGH + 1):
            distance = shift - arrived_eighth.astype(jnp.float32) * 0.125
            weight = (jnp.exp(-0.5 * distance * distance) * density).astype(jnp.bfloat16)
            index = (arrived_plane + (shift + SPREAD_HIGH)) * KY + arrived_ky
            hit = (dest_index == index[None, :]) & tag_ok[None, :]
            weights = jnp.where(hit, weight[None, :], weights)
        padded = padded + jnp.dot(weights, arrived_rows[p], preferred_element_type=jnp.float32)
    padded = padded.reshape(slots, KY, total_cols)

    me = lax.axis_index("slab")
    forward = [(i, i + 1) for i in range(count_slab - 1)]
    backward = [(i + 1, i) for i in range(count_slab - 1)]
    from_lower = lax.ppermute(padded[slots - HALO:], "slab", forward)
    from_upper = lax.ppermute(padded[:HALO], "slab", backward)
    window = padded[1:slots - 1]
    wide = z_dev + 2 * REG_ITERS
    gridded = window.at[:HALO].add(from_lower).at[wide - HALO:].add(from_upper)
    plane_global = me * z_dev + jnp.arange(wide, dtype=jnp.int32) - REG_ITERS
    inside = ((plane_global >= 0) & (plane_global < nz))[:, None, None]
    gridded = jnp.where(inside, gridded, 0.0)
    iterate = gridded
    for sweep in range(REG_ITERS):
        centre = iterate[1:-1]
        target = gridded[sweep + 1:wide - sweep - 1]
        iterate = centre - 0.25 * (
            centre - target + (2.0 * centre - iterate[:-2] - iterate[2:])
        )
        iterate = jnp.where(inside[sweep + 1:wide - sweep - 1], iterate, 0.0)
    return (iterate[:, :, :cols], iterate[:, :, cols:])


def solution(mesh):
    placed = (P("slab", "ang", None), P("slab", None), P("slab", None), P("slab", None))
    return jax.shard_map(
        on_device,
        mesh=mesh,
        in_specs=placed,
        out_specs=(P("slab", None, "ang"), P("slab", None, "ang")),
        check_vma=False,
    )
```

```python
import math

import jax
import jax.numpy as jnp
from jax import lax
from jax.sharding import PartitionSpec as P

KY = 8
NZ = 1024
REG_ITERS = 2
SPREAD_LOW = 2
SPREAD_HIGH = 3
HALO = SPREAD_LOW + SPREAD_HIGH
CHUNKS = 4


def phase_parts(rows, cols, length):
    row_index = jnp.arange(rows, dtype=jnp.int32)[:, None]
    column = cols[None, :]
    phase_angle = (row_index * column % length).astype(jnp.float32) * (2.0 * math.pi / length)
    return jnp.cos(phase_angle), jnp.sin(phase_angle)


def dft_table(length, groups):
    split = 1 << (int(math.log2(length)) // 2)
    cos_hi, sin_hi = phase_parts(length, jnp.arange(length // split, dtype=jnp.int32) * split, length)
    cos_lo, sin_lo = phase_parts(length, jnp.arange(split, dtype=jnp.int32), length)
    shape = (length, groups, 1, length // split // groups, 1)
    a, b = cos_hi.reshape(shape), sin_hi.reshape(shape)
    c, d = cos_lo.reshape(length, 1, 1, 1, split), sin_lo.reshape(length, 1, 1, 1, split)
    is_re = (jnp.arange(2, dtype=jnp.int32) == 0).reshape(1, 1, 2, 1, 1)
    table = jnp.where(is_re, a * c - b * d, -(b * c + a * d))
    return table.reshape(length, groups, 2, length // groups)


def on_device(projections, dest_plane, sub_offset, ky_bin):
    count_ang = lax.axis_size("ang")
    count_slab = lax.axis_size("slab")
    local_count, quarter, full_width = projections.shape
    height = quarter * count_ang
    cols = full_width // count_ang
    total_cols = 2 * cols
    nz = NZ
    z_dev = nz // count_slab
    per_proj = 2 * z_dev
    chunks = CHUNKS
    width = cols // chunks

    edges = jnp.arange(count_slab + 1, dtype=jnp.int32) * z_dev
    start = jnp.sum((dest_plane[:, None, :] < edges[None, :, None]).astype(jnp.int32), axis=2)
    counts = start[:, 1:] - start[:, :-1]
    slot = jnp.arange(per_proj, dtype=jnp.int32)
    valid = slot[None, None, :] < counts[:, :, None]
    row_q = (start[:, :-1, None] + slot[None, None, :] + height // 2) % height
    q_iota = jnp.arange(height, dtype=jnp.int32)
    select = ((row_q[..., None] == q_iota) & valid[..., None]).astype(jnp.bfloat16)
    label_cols = jnp.stack(
        [dest_plane % z_dev, sub_offset, ky_bin, jnp.ones_like(ky_bin)], axis=-1
    ).astype(jnp.bfloat16)
    labels = jnp.einsum("pbjq,pqk->bpjk", select, label_cols, preferred_element_type=jnp.float32)
    arrived_labels = lax.all_to_all(labels, "slab", split_axis=0, concat_axis=0, tiled=True)

    table = dft_table(full_width, count_ang).astype(jnp.bfloat16).reshape(full_width, count_ang, total_cols)
    transformed = jnp.einsum(
        "rw,wdk->drk",
        projections.reshape(local_count * quarter, full_width),
        table,
        preferred_element_type=jnp.float32,
    ).astype(jnp.bfloat16)
    received = lax.all_to_all(transformed, "ang", split_axis=0, concat_axis=0, tiled=True)
    received = received.reshape(count_ang, local_count, quarter, 2, chunks, width)
    lhs = dft_table(height, 1).reshape(height, 2, height)
    lhs = jnp.concatenate([lhs[:, 0], -lhs[:, 1]], axis=1).astype(jnp.bfloat16)
    lhs = lhs.reshape(height, 2, count_ang, quarter)
    unitary = 1.0 / math.sqrt(height * full_width)

    density = 1.0 / math.sqrt(local_count * count_slab)
    slots = z_dev + HALO + 1
    tags = arrived_labels.reshape(-1, 4)
    arrived_plane = tags[:, 0].astype(jnp.int32)
    arrived_eighth = tags[:, 1].astype(jnp.int32)
    arrived_ky = tags[:, 2].astype(jnp.int32)
    tag_ok = tags[:, 3] > 0.5
    dest_index = jnp.arange(slots * KY, dtype=jnp.int32)[:, None]
    weights = jnp.zeros((slots * KY, tags.shape[0]), jnp.bfloat16)
    for shift in range(-SPREAD_LOW, SPREAD_HIGH + 1):
        distance = shift - arrived_eighth.astype(jnp.float32) * 0.125
        weight = (jnp.exp(-0.5 * distance * distance) * density).astype(jnp.bfloat16)
        index = (arrived_plane + (shift + SPREAD_HIGH)) * KY + arrived_ky
        hit = (dest_index == index[None, :]) & tag_ok[None, :]
        weights = jnp.where(hit, weight[None, :], weights)

    pieces = []
    for chunk in range(chunks):
        real_in = received[:, :, :, 0, chunk]
        imag_in = received[:, :, :, 1, chunk]
        rhs = jnp.stack(
            [jnp.concatenate([real_in, imag_in], axis=-1), jnp.concatenate([imag_in, -real_in], axis=-1)],
            axis=0,
        )
        spectrum = jnp.einsum("qcsh,csphn->pqn", lhs, rhs, preferred_element_type=jnp.float32)
        spectrum = (spectrum * unitary).astype(jnp.bfloat16)
        packed = jnp.einsum("pbjq,pqn->bpjn", select, spectrum, preferred_element_type=jnp.bfloat16)
        arrived = lax.all_to_all(packed, "slab", split_axis=0, concat_axis=0, tiled=True)
        grid = jnp.dot(weights, arrived.reshape(-1, 2 * width), preferred_element_type=jnp.float32)
        pieces.append(grid.reshape(slots, KY, 2, width))
    padded = jnp.stack(pieces, axis=3).reshape(slots, KY, total_cols)

    me = lax.axis_index("slab")
    forward = [(i, i + 1) for i in range(count_slab - 1)]
    backward = [(i + 1, i) for i in range(count_slab - 1)]
    from_lower = lax.ppermute(padded[slots - HALO:], "slab", forward)
    from_upper = lax.ppermute(padded[:HALO], "slab", backward)
    window = padded[1:slots - 1]
    wide = z_dev + 2 * REG_ITERS
    gridded = window.at[:HALO].add(from_lower).at[wide - HALO:].add(from_upper)
    plane_global = me * z_dev + jnp.arange(wide, dtype=jnp.int32) - REG_ITERS
    inside = ((plane_global >= 0) & (plane_global < nz))[:, None, None]
    gridded = jnp.where(inside, gridded, 0.0)
    iterate = gridded
    for sweep in range(REG_ITERS):
        centre = iterate[1:-1]
        target = gridded[sweep + 1:wide - sweep - 1]
        iterate = centre - 0.25 * (
            centre - target + (2.0 * centre - iterate[:-2] - iterate[2:])
        )
        iterate = jnp.where(inside[sweep + 1:wide - sweep - 1], iterate, 0.0)
    return (iterate[:, :, :cols], iterate[:, :, cols:])


def solution(mesh):
    placed = (P("slab", "ang", None), P("slab", None), P("slab", None), P("slab", None))
    return jax.shard_map(
        on_device,
        mesh=mesh,
        in_specs=placed,
        out_specs=(P("slab", None, "ang"), P("slab", None, "ang")),
        check_vma=False,
    )
```

```python
import math

import jax
import jax.numpy as jnp
from jax import lax
from jax.sharding import PartitionSpec as P

KY = 8
NZ = 1024
REG_ITERS = 2
SPREAD_LOW = 2
SPREAD_HIGH = 3
HALO = SPREAD_LOW + SPREAD_HIGH
CHUNKS = 4


def phase_parts(rows, cols, length):
    row_index = jnp.arange(rows, dtype=jnp.int32)[:, None]
    column = cols[None, :]
    phase_angle = (row_index * column % length).astype(jnp.float32) * (2.0 * math.pi / length)
    return jnp.cos(phase_angle), jnp.sin(phase_angle)


def dft_block(rows, col_hi, length):
    split = 1 << (int(math.log2(length)) // 2)
    cos_hi, sin_hi = phase_parts(rows, col_hi * split, length)
    cos_lo, sin_lo = phase_parts(rows, jnp.arange(split, dtype=jnp.int32), length)
    a, b = cos_hi[:, :, None, None], sin_hi[:, :, None, None]
    c, d = cos_lo[:, None, None, :], sin_lo[:, None, None, :]
    is_re = (jnp.arange(2, dtype=jnp.int32) == 0).reshape(1, 1, 2, 1)
    return jnp.where(is_re, a * c - b * d, -(b * c + a * d)), split


def on_device(projections, dest_plane, sub_offset, ky_bin):
    count_ang = lax.axis_size("ang")
    count_slab = lax.axis_size("slab")
    local_count, quarter, full_width = projections.shape
    height = quarter * count_ang
    cols = full_width // count_ang
    total_cols = 2 * cols
    nz = NZ
    z_dev = nz // count_slab
    per_proj = 2 * z_dev
    me_ang = lax.axis_index("ang")

    edges = jnp.arange(count_slab + 1, dtype=jnp.int32) * z_dev
    start = jnp.sum((dest_plane[:, None, :] < edges[None, :, None]).astype(jnp.int32), axis=2)
    counts = start[:, 1:] - start[:, :-1]
    slot = jnp.arange(per_proj, dtype=jnp.int32)
    valid = slot[None, None, :] < counts[:, :, None]
    row_q = (start[:, :-1, None] + slot[None, None, :] + height // 2) % height
    q_iota = jnp.arange(height, dtype=jnp.int32)
    select = ((row_q[..., None] == q_iota) & valid[..., None]).astype(jnp.bfloat16)
    label_cols = jnp.stack(
        [dest_plane % z_dev, sub_offset, ky_bin, jnp.ones_like(ky_bin)], axis=-1
    ).astype(jnp.bfloat16)
    labels = jnp.einsum("pbjq,pqk->bpjk", select, label_cols, preferred_element_type=jnp.float32)
    arrived_labels = lax.all_to_all(labels, "slab", split_axis=0, concat_axis=0, tiled=True)

    split_w = 1 << (int(math.log2(full_width)) // 2)
    per_block = cols // split_w
    col_hi = ((jnp.arange(count_ang, dtype=jnp.int32)[:, None] + me_ang) % count_ang) * per_block
    col_hi = (col_hi + jnp.arange(per_block, dtype=jnp.int32)[None, :]).reshape(-1)
    table, _ = dft_block(full_width, col_hi, full_width)
    table = table.reshape(full_width, count_ang, per_block, 2, split_w)
    table = jnp.transpose(table, (0, 1, 3, 2, 4)).astype(jnp.bfloat16)
    table = table.reshape(full_width, count_ang, total_cols)
    transformed = jnp.einsum(
        "rw,wdk->drk",
        projections.reshape(local_count * quarter, full_width),
        table,
        preferred_element_type=jnp.float32,
    ).astype(jnp.bfloat16)
    blocks = [transformed[0]]
    for shift in range(1, count_ang):
        pairs = [(i, (i + shift) % count_ang) for i in range(count_ang)]
        blocks.append(lax.ppermute(transformed[shift], "ang", pairs))
    received = jnp.stack(blocks).reshape(count_ang, local_count, quarter, total_cols)

    split_h = 1 << (int(math.log2(height)) // 2)
    per_quarter = quarter // split_h
    h_hi = ((me_ang - jnp.arange(count_ang, dtype=jnp.int32)[:, None]) % count_ang) * per_quarter
    h_hi = (h_hi + jnp.arange(per_quarter, dtype=jnp.int32)[None, :]).reshape(-1)
    lhs, _ = dft_block(height, h_hi, height)
    lhs = lhs.reshape(height, count_ang, per_quarter, 2, split_h)
    lhs = jnp.where((jnp.arange(2) == 0).reshape(1, 1, 1, 2, 1), lhs, -lhs)
    lhs = jnp.transpose(lhs, (0, 3, 1, 2, 4)).astype(jnp.bfloat16)
    lhs = lhs.reshape(height, 2, count_ang, quarter)
    unitary = 1.0 / math.sqrt(height * full_width)
    real_in = received[..., :cols]
    imag_in = received[..., cols:]
    rhs = jnp.stack(
        [received, jnp.concatenate([imag_in, -real_in], axis=-1)], axis=0
    )
    spectrum = jnp.einsum("qcsh,csphn->pqn", lhs, rhs, preferred_element_type=jnp.float32)
    spectrum = (spectrum * unitary).astype(jnp.bfloat16)
    packed = jnp.einsum("pbjq,pqn->bpjn", select, spectrum, preferred_element_type=jnp.bfloat16)
    arrived = lax.all_to_all(packed, "slab", split_axis=0, concat_axis=0, tiled=True)

    density = 1.0 / math.sqrt(local_count * count_slab)
    slots = z_dev + HALO + 1
    tags = arrived_labels.reshape(-1, 4)
    arrived_plane = tags[:, 0].astype(jnp.int32)
    arrived_eighth = tags[:, 1].astype(jnp.int32)
    arrived_ky = tags[:, 2].astype(jnp.int32)
    tag_ok = tags[:, 3] > 0.5
    dest_index = jnp.arange(slots * KY, dtype=jnp.int32)[:, None]
    weights = jnp.zeros((slots * KY, tags.shape[0]), jnp.bfloat16)
    for shift in range(-SPREAD_LOW, SPREAD_HIGH + 1):
        distance = shift - arrived_eighth.astype(jnp.float32) * 0.125
        weight = (jnp.exp(-0.5 * distance * distance) * density).astype(jnp.bfloat16)
        index = (arrived_plane + (shift + SPREAD_HIGH)) * KY + arrived_ky
        hit = (dest_index == index[None, :]) & tag_ok[None, :]
        weights = jnp.where(hit, weight[None, :], weights)

    padded = jnp.dot(weights, arrived.reshape(-1, total_cols), preferred_element_type=jnp.float32)
    padded = padded.reshape(slots, KY, total_cols)

    me = lax.axis_index("slab")
    forward = [(i, i + 1) for i in range(count_slab - 1)]
    backward = [(i + 1, i) for i in range(count_slab - 1)]
    from_lower = lax.ppermute(padded[slots - HALO:], "slab", forward)
    from_upper = lax.ppermute(padded[:HALO], "slab", backward)
    window = padded[1:slots - 1]
    wide = z_dev + 2 * REG_ITERS
    gridded = window.at[:HALO].add(from_lower).at[wide - HALO:].add(from_upper)
    plane_global = me * z_dev + jnp.arange(wide, dtype=jnp.int32) - REG_ITERS
    inside = ((plane_global >= 0) & (plane_global < nz))[:, None, None]
    gridded = jnp.where(inside, gridded, 0.0)
    iterate = gridded
    for sweep in range(REG_ITERS):
        centre = iterate[1:-1]
        target = gridded[sweep + 1:wide - sweep - 1]
        iterate = centre - 0.25 * (
            centre - target + (2.0 * centre - iterate[:-2] - iterate[2:])
        )
        iterate = jnp.where(inside[sweep + 1:wide - sweep - 1], iterate, 0.0)
    return (iterate[:, :, :cols], iterate[:, :, cols:])


def solution(mesh):
    placed = (P("slab", "ang", None), P("slab", None), P("slab", None), P("slab", None))
    return jax.shard_map(
        on_device,
        mesh=mesh,
        in_specs=placed,
        out_specs=(P("slab", None, "ang"), P("slab", None, "ang")),
        check_vma=False,
    )
```

```python
import math

import jax
import jax.numpy as jnp
from jax import lax
from jax.sharding import PartitionSpec as P

KY = 8
NZ = 1024
REG_ITERS = 2
SPREAD_LOW = 2
SPREAD_HIGH = 3
HALO = SPREAD_LOW + SPREAD_HIGH
CHUNKS = 4


def phase_parts(rows, cols, length):
    row_index = jnp.arange(rows, dtype=jnp.int32)[:, None]
    column = cols[None, :]
    phase_angle = (row_index * column % length).astype(jnp.float32) * (2.0 * math.pi / length)
    return jnp.cos(phase_angle), jnp.sin(phase_angle)


def dft_block(rows, col_hi, length):
    split = 1 << (int(math.log2(length)) // 2)
    cos_hi, sin_hi = phase_parts(rows, col_hi * split, length)
    cos_lo, sin_lo = phase_parts(rows, jnp.arange(split, dtype=jnp.int32), length)
    a, b = cos_hi[:, :, None, None], sin_hi[:, :, None, None]
    c, d = cos_lo[:, None, None, :], sin_lo[:, None, None, :]
    is_re = (jnp.arange(2, dtype=jnp.int32) == 0).reshape(1, 1, 2, 1)
    return jnp.where(is_re, a * c - b * d, -(b * c + a * d)), split


def on_device(projections, dest_plane, sub_offset, ky_bin):
    count_ang = lax.axis_size("ang")
    count_slab = lax.axis_size("slab")
    local_count, quarter, full_width = projections.shape
    height = quarter * count_ang
    cols = full_width // count_ang
    total_cols = 2 * cols
    nz = NZ
    z_dev = nz // count_slab
    per_proj = 2 * z_dev
    me_ang = lax.axis_index("ang")

    edges = jnp.arange(count_slab + 1, dtype=jnp.int32) * z_dev
    start = jnp.sum((dest_plane[:, None, :] < edges[None, :, None]).astype(jnp.int32), axis=2)
    counts = start[:, 1:] - start[:, :-1]
    slot = jnp.arange(per_proj, dtype=jnp.int32)
    valid = slot[None, None, :] < counts[:, :, None]
    row_q = (start[:, :-1, None] + slot[None, None, :] + height // 2) % height
    q_iota = jnp.arange(height, dtype=jnp.int32)
    select = ((row_q[..., None] == q_iota) & valid[..., None]).astype(jnp.bfloat16)
    label_cols = jnp.stack(
        [dest_plane % z_dev, sub_offset, ky_bin, jnp.ones_like(ky_bin)], axis=-1
    ).astype(jnp.bfloat16)
    labels = jnp.einsum("pbjq,pqk->bpjk", select, label_cols, preferred_element_type=jnp.float32)
    arrived_labels = lax.all_to_all(labels, "slab", split_axis=0, concat_axis=0, tiled=True)

    split_w = 1 << (int(math.log2(full_width)) // 2)
    per_block = cols // split_w
    col_hi = ((jnp.arange(count_ang, dtype=jnp.int32)[:, None] + me_ang) % count_ang) * per_block
    col_hi = (col_hi + jnp.arange(per_block, dtype=jnp.int32)[None, :]).reshape(-1)
    table, _ = dft_block(full_width, col_hi, full_width)
    table = table.reshape(full_width, count_ang, per_block, 2, split_w)
    table = jnp.transpose(table, (0, 1, 3, 2, 4)).astype(jnp.bfloat16)
    table = table.reshape(full_width, count_ang, total_cols)

    split_h = 1 << (int(math.log2(height)) // 2)
    per_quarter = quarter // split_h
    h_hi = ((me_ang - jnp.arange(count_ang, dtype=jnp.int32)[:, None]) % count_ang) * per_quarter
    h_hi = (h_hi + jnp.arange(per_quarter, dtype=jnp.int32)[None, :]).reshape(-1)
    lhs, _ = dft_block(height, h_hi, height)
    lhs = lhs.reshape(height, count_ang, per_quarter, 2, split_h)
    lhs = jnp.where((jnp.arange(2) == 0).reshape(1, 1, 1, 2, 1), lhs, -lhs)
    lhs = jnp.transpose(lhs, (0, 3, 1, 2, 4)).astype(jnp.bfloat16)
    lhs = lhs.reshape(height, 2 * height)
    unitary = 1.0 / math.sqrt(height * full_width)

    arrived_rows = []
    held = None
    for p in range(local_count):
        blocks = [
            jnp.dot(projections[p], table[:, shift], preferred_element_type=jnp.float32).astype(jnp.bfloat16)
            for shift in range(count_ang)
        ]
        if held is not None:
            blocks, held = lax.optimization_barrier((blocks, held))
        received = [blocks[0]]
        for shift in range(1, count_ang):
            pairs = [(i, (i + shift) % count_ang) for i in range(count_ang)]
            received.append(lax.ppermute(blocks[shift], "ang", pairs))
        held = received
        direct = jnp.concatenate(received, axis=0)
        swapped = jnp.concatenate([direct[:, cols:], -direct[:, :cols]], axis=1)
        rhs = jnp.concatenate([direct, swapped], axis=0)
        spectrum = jnp.dot(lhs, rhs, preferred_element_type=jnp.float32)
        spectrum = (spectrum * unitary).astype(jnp.bfloat16)
        packed = jnp.dot(
            select[p].reshape(count_slab * per_proj, height), spectrum, preferred_element_type=jnp.bfloat16
        )
        arrived_rows.append(
            lax.all_to_all(
                packed.reshape(count_slab, per_proj, total_cols), "slab", split_axis=0, concat_axis=0, tiled=True
            ).reshape(-1, total_cols)
        )

    density = 1.0 / math.sqrt(local_count * count_slab)
    slots = z_dev + HALO + 1
    dest_index = jnp.arange(slots * KY, dtype=jnp.int32)[:, None]
    padded = jnp.zeros((slots * KY, total_cols), jnp.float32)
    for p in range(local_count):
        tags = arrived_labels[:, p].reshape(-1, 4)
        arrived_plane = tags[:, 0].astype(jnp.int32)
        arrived_eighth = tags[:, 1].astype(jnp.int32)
        arrived_ky = tags[:, 2].astype(jnp.int32)
        tag_ok = tags[:, 3] > 0.5
        weights = jnp.zeros((slots * KY, tags.shape[0]), jnp.bfloat16)
        for shift in range(-SPREAD_LOW, SPREAD_HIGH + 1):
            distance = shift - arrived_eighth.astype(jnp.float32) * 0.125
            weight = (jnp.exp(-0.5 * distance * distance) * density).astype(jnp.bfloat16)
            index = (arrived_plane + (shift + SPREAD_HIGH)) * KY + arrived_ky
            hit = (dest_index == index[None, :]) & tag_ok[None, :]
            weights = jnp.where(hit, weight[None, :], weights)
        padded = padded + jnp.dot(weights, arrived_rows[p], preferred_element_type=jnp.float32)
    padded = padded.reshape(slots, KY, total_cols)

    me = lax.axis_index("slab")
    forward = [(i, i + 1) for i in range(count_slab - 1)]
    backward = [(i + 1, i) for i in range(count_slab - 1)]
    from_lower = lax.ppermute(padded[slots - HALO:], "slab", forward)
    from_upper = lax.ppermute(padded[:HALO], "slab", backward)
    window = padded[1:slots - 1]
    wide = z_dev + 2 * REG_ITERS
    gridded = window.at[:HALO].add(from_lower).at[wide - HALO:].add(from_upper)
    plane_global = me * z_dev + jnp.arange(wide, dtype=jnp.int32) - REG_ITERS
    inside = ((plane_global >= 0) & (plane_global < nz))[:, None, None]
    gridded = jnp.where(inside, gridded, 0.0)
    iterate = gridded
    for sweep in range(REG_ITERS):
        centre = iterate[1:-1]
        target = gridded[sweep + 1:wide - sweep - 1]
        iterate = centre - 0.25 * (
            centre - target + (2.0 * centre - iterate[:-2] - iterate[2:])
        )
        iterate = jnp.where(inside[sweep + 1:wide - sweep - 1], iterate, 0.0)
    return (iterate[:, :, :cols], iterate[:, :, cols:])


def solution(mesh):
    placed = (P("slab", "ang", None), P("slab", None), P("slab", None), P("slab", None))
    return jax.shard_map(
        on_device,
        mesh=mesh,
        in_specs=placed,
        out_specs=(P("slab", None, "ang"), P("slab", None, "ang")),
        check_vma=False,
    )
```

```python
import math

import jax
import jax.numpy as jnp
from jax import lax
from jax.sharding import PartitionSpec as P

KY = 8
NZ = 1024
REG_ITERS = 2
SPREAD_LOW = 2
SPREAD_HIGH = 3
HALO = SPREAD_LOW + SPREAD_HIGH
CHUNKS = 4


def phase_parts(rows, cols, length):
    row_index = jnp.arange(rows, dtype=jnp.int32)[:, None]
    column = cols[None, :]
    phase_angle = (row_index * column % length).astype(jnp.float32) * (2.0 * math.pi / length)
    return jnp.cos(phase_angle), jnp.sin(phase_angle)


def dft_block(rows, col_hi, length, shape_hi, shape_lo, part_axis, sine_sign):
    split = 1 << (int(math.log2(length)) // 2)
    cos_hi, sin_hi = phase_parts(rows, col_hi * split, length)
    cos_lo, sin_lo = phase_parts(rows, jnp.arange(split, dtype=jnp.int32), length)
    a, b = cos_hi.reshape(shape_hi), sin_hi.reshape(shape_hi)
    c, d = cos_lo.reshape(shape_lo), sin_lo.reshape(shape_lo)
    pick = [1] * len(shape_hi)
    pick[part_axis] = 2
    is_cos = (jnp.arange(2, dtype=jnp.int32) == 0).reshape(pick)
    return jnp.where(is_cos, a * c - b * d, sine_sign * (b * c + a * d))


def on_device(projections, dest_plane, sub_offset, ky_bin):
    count_ang = lax.axis_size("ang")
    count_slab = lax.axis_size("slab")
    local_count, quarter, full_width = projections.shape
    height = quarter * count_ang
    cols = full_width // count_ang
    total_cols = 2 * cols
    nz = NZ
    z_dev = nz // count_slab
    per_proj = 2 * z_dev
    me_ang = lax.axis_index("ang")

    edges = jnp.arange(count_slab + 1, dtype=jnp.int32) * z_dev
    start = jnp.sum((dest_plane[:, None, :] < edges[None, :, None]).astype(jnp.int32), axis=2)
    counts = start[:, 1:] - start[:, :-1]
    slot = jnp.arange(per_proj, dtype=jnp.int32)
    valid = slot[None, None, :] < counts[:, :, None]
    row_q = (start[:, :-1, None] + slot[None, None, :] + height // 2) % height
    q_iota = jnp.arange(height, dtype=jnp.int32)
    select = ((row_q[..., None] == q_iota) & valid[..., None]).astype(jnp.bfloat16)
    label_cols = jnp.stack(
        [dest_plane % z_dev, sub_offset, ky_bin, jnp.ones_like(ky_bin)], axis=-1
    ).astype(jnp.bfloat16)
    labels = jnp.einsum("pbjq,pqk->bpjk", select, label_cols, preferred_element_type=jnp.float32)
    arrived_labels = lax.all_to_all(labels, "slab", split_axis=0, concat_axis=0, tiled=True)

    split_w = 1 << (int(math.log2(full_width)) // 2)
    per_block = cols // split_w
    col_hi = ((jnp.arange(count_ang, dtype=jnp.int32)[:, None] + me_ang) % count_ang) * per_block
    col_hi = (col_hi + jnp.arange(per_block, dtype=jnp.int32)[None, :]).reshape(-1)
    table = dft_block(
        full_width, col_hi, full_width,
        (full_width, count_ang, 1, per_block, 1), (full_width, 1, 1, 1, split_w), 2, -1.0,
    )
    table = table.astype(jnp.bfloat16).reshape(full_width, count_ang, total_cols)

    split_h = 1 << (int(math.log2(height)) // 2)
    per_quarter = quarter // split_h
    h_hi = ((me_ang - jnp.arange(count_ang, dtype=jnp.int32)[:, None]) % count_ang) * per_quarter
    h_hi = (h_hi + jnp.arange(per_quarter, dtype=jnp.int32)[None, :]).reshape(-1)
    lhs = dft_block(
        height, h_hi, height, (height, 1, count_ang, per_quarter, 1), (height, 1, 1, 1, split_h), 1, 1.0
    )
    lhs = lhs.astype(jnp.bfloat16).reshape(height, 2 * height)
    unitary = 1.0 / math.sqrt(height * full_width)

    packs = []
    for p in range(local_count):
        blocks = [
            jnp.dot(projections[p], table[:, shift], preferred_element_type=jnp.float32).astype(jnp.bfloat16)
            for shift in range(count_ang)
        ]
        received = [blocks[0]]
        for shift in range(1, count_ang):
            pairs = [(i, (i + shift) % count_ang) for i in range(count_ang)]
            received.append(lax.ppermute(blocks[shift], "ang", pairs))
        direct = jnp.concatenate(received, axis=0)
        swapped = jnp.concatenate([direct[:, cols:], -direct[:, :cols]], axis=1)
        rhs = jnp.concatenate([direct, swapped], axis=0)
        spectrum = jnp.dot(lhs, rhs, preferred_element_type=jnp.float32)
        spectrum = (spectrum * unitary).astype(jnp.bfloat16)
        packs.append(
            jnp.dot(select[p].reshape(count_slab * per_proj, height), spectrum, preferred_element_type=jnp.bfloat16)
        )
    outgoing = jnp.concatenate(packs, axis=1).reshape(count_slab, per_proj, local_count * total_cols)
    arrived = lax.all_to_all(outgoing, "slab", split_axis=0, concat_axis=0, tiled=True)
    arrived = arrived.reshape(count_slab * per_proj, local_count, total_cols)
    arrived_rows = [arrived[:, p] for p in range(local_count)]

    density = 1.0 / math.sqrt(local_count * count_slab)
    slots = z_dev + HALO + 1
    dest_index = jnp.arange(slots * KY, dtype=jnp.int32)[:, None]
    padded = jnp.zeros((slots * KY, total_cols), jnp.float32)
    for p in range(local_count):
        tags = arrived_labels[:, p].reshape(-1, 4)
        arrived_plane = tags[:, 0].astype(jnp.int32)
        arrived_eighth = tags[:, 1].astype(jnp.int32)
        arrived_ky = tags[:, 2].astype(jnp.int32)
        tag_ok = tags[:, 3] > 0.5
        weights = jnp.zeros((slots * KY, tags.shape[0]), jnp.bfloat16)
        for shift in range(-SPREAD_LOW, SPREAD_HIGH + 1):
            distance = shift - arrived_eighth.astype(jnp.float32) * 0.125
            weight = (jnp.exp(-0.5 * distance * distance) * density).astype(jnp.bfloat16)
            index = (arrived_plane + (shift + SPREAD_HIGH)) * KY + arrived_ky
            hit = (dest_index == index[None, :]) & tag_ok[None, :]
            weights = jnp.where(hit, weight[None, :], weights)
        padded = padded + jnp.dot(weights, arrived_rows[p], preferred_element_type=jnp.float32)
    padded = padded.reshape(slots, KY, total_cols)

    me = lax.axis_index("slab")
    forward = [(i, i + 1) for i in range(count_slab - 1)]
    backward = [(i + 1, i) for i in range(count_slab - 1)]
    from_lower = lax.ppermute(padded[slots - HALO:], "slab", forward)
    from_upper = lax.ppermute(padded[:HALO], "slab", backward)
    window = padded[1:slots - 1]
    wide = z_dev + 2 * REG_ITERS
    gridded = window.at[:HALO].add(from_lower).at[wide - HALO:].add(from_upper)
    plane_global = me * z_dev + jnp.arange(wide, dtype=jnp.int32) - REG_ITERS
    inside = ((plane_global >= 0) & (plane_global < nz))[:, None, None]
    gridded = jnp.where(inside, gridded, 0.0)
    iterate = gridded
    for sweep in range(REG_ITERS):
        centre = iterate[1:-1]
        target = gridded[sweep + 1:wide - sweep - 1]
        iterate = centre - 0.25 * (
            centre - target + (2.0 * centre - iterate[:-2] - iterate[2:])
        )
        iterate = jnp.where(inside[sweep + 1:wide - sweep - 1], iterate, 0.0)
    return (iterate[:, :, :cols], iterate[:, :, cols:])


def solution(mesh):
    placed = (P("slab", "ang", None), P("slab", None), P("slab", None), P("slab", None))
    return jax.shard_map(
        on_device,
        mesh=mesh,
        in_specs=placed,
        out_specs=(P("slab", None, "ang"), P("slab", None, "ang")),
        check_vma=False,
    )
```

```python
import math

import jax
import jax.numpy as jnp
from jax import lax
from jax.sharding import PartitionSpec as P

KY = 8
NZ = 1024
REG_ITERS = 2
SPREAD_LOW = 2
SPREAD_HIGH = 3
HALO = SPREAD_LOW + SPREAD_HIGH
CHUNKS = 4


def phase_parts(rows, cols, length):
    row_index = jnp.arange(rows, dtype=jnp.int32)[:, None]
    column = cols[None, :]
    phase_angle = (row_index * column % length).astype(jnp.float32) * (2.0 * math.pi / length)
    return jnp.cos(phase_angle), jnp.sin(phase_angle)


def dft_block(rows, col_hi, length):
    split = 1 << (int(math.log2(length)) // 2)
    cos_hi, sin_hi = phase_parts(rows, col_hi * split, length)
    cos_lo, sin_lo = phase_parts(rows, jnp.arange(split, dtype=jnp.int32), length)
    a, b = cos_hi[:, :, None, None], sin_hi[:, :, None, None]
    c, d = cos_lo[:, None, None, :], sin_lo[:, None, None, :]
    is_re = (jnp.arange(2, dtype=jnp.int32) == 0).reshape(1, 1, 2, 1)
    return jnp.where(is_re, a * c - b * d, -(b * c + a * d)), split


def on_device(projections, dest_plane, sub_offset, ky_bin):
    count_ang = lax.axis_size("ang")
    count_slab = lax.axis_size("slab")
    local_count, quarter, full_width = projections.shape
    height = quarter * count_ang
    cols = full_width // count_ang
    total_cols = 2 * cols
    nz = NZ
    z_dev = nz // count_slab
    per_proj = 2 * z_dev
    me_ang = lax.axis_index("ang")

    edges = jnp.arange(count_slab + 1, dtype=jnp.int32) * z_dev
    start = jnp.sum((dest_plane[:, None, :] < edges[None, :, None]).astype(jnp.int32), axis=2)
    counts = start[:, 1:] - start[:, :-1]
    slot = jnp.arange(per_proj, dtype=jnp.int32)
    valid = slot[None, None, :] < counts[:, :, None]
    row_q = (start[:, :-1, None] + slot[None, None, :] + height // 2) % height
    q_iota = jnp.arange(height, dtype=jnp.int32)
    select = ((row_q[..., None] == q_iota) & valid[..., None]).astype(jnp.bfloat16)
    label_cols = jnp.stack(
        [dest_plane % z_dev, sub_offset, ky_bin, jnp.ones_like(ky_bin)], axis=-1
    ).astype(jnp.bfloat16)
    labels = jnp.einsum("pbjq,pqk->bpjk", select, label_cols, preferred_element_type=jnp.float32)
    arrived_labels = lax.all_to_all(labels, "slab", split_axis=0, concat_axis=0, tiled=True)

    split_w = 1 << (int(math.log2(full_width)) // 2)
    per_block = cols // split_w
    col_hi = ((jnp.arange(count_ang, dtype=jnp.int32)[:, None] + me_ang) % count_ang) * per_block
    col_hi = (col_hi + jnp.arange(per_block, dtype=jnp.int32)[None, :]).reshape(-1)
    table, _ = dft_block(full_width, col_hi, full_width)
    table = table.reshape(full_width, count_ang, per_block, 2, split_w)
    table = jnp.transpose(table, (0, 1, 3, 2, 4)).astype(jnp.bfloat16)
    table = table.reshape(full_width, count_ang, total_cols)

    split_h = 1 << (int(math.log2(height)) // 2)
    per_quarter = quarter // split_h
    h_hi = ((me_ang - jnp.arange(count_ang, dtype=jnp.int32)[:, None]) % count_ang) * per_quarter
    h_hi = (h_hi + jnp.arange(per_quarter, dtype=jnp.int32)[None, :]).reshape(-1)
    lhs, _ = dft_block(height, h_hi, height)
    lhs = lhs.reshape(height, count_ang, per_quarter, 2, split_h)
    lhs = jnp.where((jnp.arange(2) == 0).reshape(1, 1, 1, 2, 1), lhs, -lhs)
    lhs = jnp.transpose(lhs, (0, 3, 1, 2, 4)).astype(jnp.bfloat16)
    lhs = lhs.reshape(height, 2 * height)
    unitary = 1.0 / math.sqrt(height * full_width)

    arrived_rows = []
    held = None
    for p in range(local_count):
        image = projections[p]
        if held is not None:
            image, held = lax.optimization_barrier((image, held))
        blocks = [
            jnp.dot(image, table[:, shift], preferred_element_type=jnp.float32).astype(jnp.bfloat16)
            for shift in range(count_ang)
        ]
        received = [blocks[0]]
        for shift in range(1, count_ang):
            pairs = [(i, (i + shift) % count_ang) for i in range(count_ang)]
            received.append(lax.ppermute(blocks[shift], "ang", pairs))
        direct = jnp.concatenate(received, axis=0)
        swapped = jnp.concatenate([direct[:, cols:], -direct[:, :cols]], axis=1)
        rhs = jnp.concatenate([direct, swapped], axis=0)
        spectrum = jnp.dot(lhs, rhs, preferred_element_type=jnp.float32)
        spectrum = (spectrum * unitary).astype(jnp.bfloat16)
        packed = jnp.dot(
            select[p].reshape(count_slab * per_proj, height), spectrum, preferred_element_type=jnp.bfloat16
        )
        held = packed
        arrived_rows.append(
            lax.all_to_all(
                packed.reshape(count_slab, per_proj, total_cols), "slab", split_axis=0, concat_axis=0, tiled=True
            ).reshape(-1, total_cols)
        )

    density = 1.0 / math.sqrt(local_count * count_slab)
    slots = z_dev + HALO + 1
    dest_index = jnp.arange(slots * KY, dtype=jnp.int32)[:, None]
    padded = jnp.zeros((slots * KY, total_cols), jnp.float32)
    for p in range(local_count):
        tags = arrived_labels[:, p].reshape(-1, 4)
        arrived_plane = tags[:, 0].astype(jnp.int32)
        arrived_eighth = tags[:, 1].astype(jnp.int32)
        arrived_ky = tags[:, 2].astype(jnp.int32)
        tag_ok = tags[:, 3] > 0.5
        weights = jnp.zeros((slots * KY, tags.shape[0]), jnp.bfloat16)
        for shift in range(-SPREAD_LOW, SPREAD_HIGH + 1):
            distance = shift - arrived_eighth.astype(jnp.float32) * 0.125
            weight = (jnp.exp(-0.5 * distance * distance) * density).astype(jnp.bfloat16)
            index = (arrived_plane + (shift + SPREAD_HIGH)) * KY + arrived_ky
            hit = (dest_index == index[None, :]) & tag_ok[None, :]
            weights = jnp.where(hit, weight[None, :], weights)
        padded = padded + jnp.dot(weights, arrived_rows[p], preferred_element_type=jnp.float32)
    padded = padded.reshape(slots, KY, total_cols)

    me = lax.axis_index("slab")
    forward = [(i, i + 1) for i in range(count_slab - 1)]
    backward = [(i + 1, i) for i in range(count_slab - 1)]
    from_lower = lax.ppermute(padded[slots - HALO:], "slab", forward)
    from_upper = lax.ppermute(padded[:HALO], "slab", backward)
    window = padded[1:slots - 1]
    wide = z_dev + 2 * REG_ITERS
    gridded = window.at[:HALO].add(from_lower).at[wide - HALO:].add(from_upper)
    plane_global = me * z_dev + jnp.arange(wide, dtype=jnp.int32) - REG_ITERS
    inside = ((plane_global >= 0) & (plane_global < nz))[:, None, None]
    gridded = jnp.where(inside, gridded, 0.0)
    iterate = gridded
    for sweep in range(REG_ITERS):
        centre = iterate[1:-1]
        target = gridded[sweep + 1:wide - sweep - 1]
        iterate = centre - 0.25 * (
            centre - target + (2.0 * centre - iterate[:-2] - iterate[2:])
        )
        iterate = jnp.where(inside[sweep + 1:wide - sweep - 1], iterate, 0.0)
    return (iterate[:, :, :cols], iterate[:, :, cols:])


def solution(mesh):
    placed = (P("slab", "ang", None), P("slab", None), P("slab", None), P("slab", None))
    return jax.shard_map(
        on_device,
        mesh=mesh,
        in_specs=placed,
        out_specs=(P("slab", None, "ang"), P("slab", None, "ang")),
        check_vma=False,
    )
```

```python
import math

import jax
import jax.numpy as jnp
from jax import lax
from jax.sharding import PartitionSpec as P

KY = 8
NZ = 1024
REG_ITERS = 2
SPREAD_LOW = 2
SPREAD_HIGH = 3
HALO = SPREAD_LOW + SPREAD_HIGH
CHUNKS = 4


def phase_parts(rows, cols, length):
    row_index = jnp.arange(rows, dtype=jnp.int32)[:, None]
    column = cols[None, :]
    phase_angle = (row_index * column % length).astype(jnp.float32) * (2.0 * math.pi / length)
    return jnp.cos(phase_angle), jnp.sin(phase_angle)


def dft_block(rows, col_hi, length):
    split = 1 << (int(math.log2(length)) // 2)
    cos_hi, sin_hi = phase_parts(rows, col_hi * split, length)
    cos_lo, sin_lo = phase_parts(rows, jnp.arange(split, dtype=jnp.int32), length)
    a, b = cos_hi[:, :, None, None], sin_hi[:, :, None, None]
    c, d = cos_lo[:, None, None, :], sin_lo[:, None, None, :]
    is_re = (jnp.arange(2, dtype=jnp.int32) == 0).reshape(1, 1, 2, 1)
    return jnp.where(is_re, a * c - b * d, -(b * c + a * d)), split


def on_device(projections, dest_plane, sub_offset, ky_bin):
    count_ang = lax.axis_size("ang")
    count_slab = lax.axis_size("slab")
    local_count, quarter, full_width = projections.shape
    height = quarter * count_ang
    cols = full_width // count_ang
    total_cols = 2 * cols
    nz = NZ
    z_dev = nz // count_slab
    per_proj = 2 * z_dev
    me_ang = lax.axis_index("ang")

    edges = jnp.arange(count_slab + 1, dtype=jnp.int32) * z_dev
    start = jnp.sum((dest_plane[:, None, :] < edges[None, :, None]).astype(jnp.int32), axis=2)
    counts = start[:, 1:] - start[:, :-1]
    slot = jnp.arange(per_proj, dtype=jnp.int32)
    valid = slot[None, None, :] < counts[:, :, None]
    row_q = (start[:, :-1, None] + slot[None, None, :] + height // 2) % height
    q_iota = jnp.arange(height, dtype=jnp.int32)
    select = ((row_q[..., None] == q_iota) & valid[..., None]).astype(jnp.bfloat16)
    label_cols = jnp.stack(
        [dest_plane % z_dev, sub_offset, ky_bin, jnp.ones_like(ky_bin)], axis=-1
    ).astype(jnp.bfloat16)
    labels = jnp.einsum("pbjq,pqk->bpjk", select, label_cols, preferred_element_type=jnp.float32)
    labels = labels.astype(jnp.int32)
    codes = jnp.where(
        labels[..., 3] > 0, (labels[..., 0] * 8 + labels[..., 1]) * KY + labels[..., 2], -1
    )
    me_slab = lax.axis_index("slab")
    every_code = lax.all_gather(codes, "slab")
    arrived_codes = lax.dynamic_index_in_dim(every_code, me_slab, axis=1, keepdims=False)

    split_w = 1 << (int(math.log2(full_width)) // 2)
    per_block = cols // split_w
    col_hi = ((jnp.arange(count_ang, dtype=jnp.int32)[:, None] + me_ang) % count_ang) * per_block
    col_hi = (col_hi + jnp.arange(per_block, dtype=jnp.int32)[None, :]).reshape(-1)
    table, _ = dft_block(full_width, col_hi, full_width)
    table = table.reshape(full_width, count_ang, per_block, 2, split_w)
    table = jnp.transpose(table, (0, 1, 3, 2, 4)).astype(jnp.bfloat16)
    table = table.reshape(full_width, count_ang, total_cols)

    split_h = 1 << (int(math.log2(height)) // 2)
    per_quarter = quarter // split_h
    h_hi = ((me_ang - jnp.arange(count_ang, dtype=jnp.int32)[:, None]) % count_ang) * per_quarter
    h_hi = (h_hi + jnp.arange(per_quarter, dtype=jnp.int32)[None, :]).reshape(-1)
    lhs, _ = dft_block(height, h_hi, height)
    lhs = lhs.reshape(height, count_ang, per_quarter, 2, split_h)
    lhs = jnp.where((jnp.arange(2) == 0).reshape(1, 1, 1, 2, 1), lhs, -lhs)
    lhs = jnp.transpose(lhs, (0, 3, 1, 2, 4)).astype(jnp.bfloat16)
    lhs = lhs.reshape(height, 2 * height)
    unitary = 1.0 / math.sqrt(height * full_width)

    arrived_rows = []
    held = None
    for p in range(local_count):
        image = projections[p]
        if held is not None:
            image, held = lax.optimization_barrier((image, held))
        blocks = [
            jnp.dot(image, table[:, shift], preferred_element_type=jnp.float32).astype(jnp.bfloat16)
            for shift in range(count_ang)
        ]
        received = [blocks[0]]
        for shift in range(1, count_ang):
            pairs = [(i, (i + shift) % count_ang) for i in range(count_ang)]
            received.append(lax.ppermute(blocks[shift], "ang", pairs))
        direct = jnp.concatenate(received, axis=0)
        swapped = jnp.concatenate([direct[:, cols:], -direct[:, :cols]], axis=1)
        rhs = jnp.concatenate([direct, swapped], axis=0)
        spectrum = jnp.dot(lhs, rhs, preferred_element_type=jnp.float32)
        spectrum = (spectrum * unitary).astype(jnp.bfloat16)
        packed = jnp.dot(
            select[p].reshape(count_slab * per_proj, height), spectrum, preferred_element_type=jnp.bfloat16
        )
        held = packed
        arrived_rows.append(
            lax.all_to_all(
                packed.reshape(count_slab, per_proj, total_cols), "slab", split_axis=0, concat_axis=0, tiled=True
            ).reshape(-1, total_cols)
        )

    density = 1.0 / math.sqrt(local_count * count_slab)
    slots = z_dev + HALO + 1
    dest_index = jnp.arange(slots * KY, dtype=jnp.int32)[:, None]
    padded = jnp.zeros((slots * KY, total_cols), jnp.float32)
    for p in range(local_count):
        code = arrived_codes[:, p].reshape(-1)
        tag_ok = code >= 0
        tag = jnp.maximum(code, 0)
        arrived_ky = tag % KY
        arrived_eighth = tag // KY % 8
        arrived_plane = tag // (8 * KY)
        weights = jnp.zeros((slots * KY, code.shape[0]), jnp.bfloat16)
        for shift in range(-SPREAD_LOW, SPREAD_HIGH + 1):
            distance = shift - arrived_eighth.astype(jnp.float32) * 0.125
            weight = (jnp.exp(-0.5 * distance * distance) * density).astype(jnp.bfloat16)
            index = (arrived_plane + (shift + SPREAD_HIGH)) * KY + arrived_ky
            hit = (dest_index == index[None, :]) & tag_ok[None, :]
            weights = jnp.where(hit, weight[None, :], weights)
        padded = padded + jnp.dot(weights, arrived_rows[p], preferred_element_type=jnp.float32)
    padded = padded.reshape(slots, KY, total_cols)

    me = lax.axis_index("slab")
    forward = [(i, i + 1) for i in range(count_slab - 1)]
    backward = [(i + 1, i) for i in range(count_slab - 1)]
    from_lower = lax.ppermute(padded[slots - HALO:], "slab", forward)
    from_upper = lax.ppermute(padded[:HALO], "slab", backward)
    window = padded[1:slots - 1]
    wide = z_dev + 2 * REG_ITERS
    gridded = window.at[:HALO].add(from_lower).at[wide - HALO:].add(from_upper)
    plane_global = me * z_dev + jnp.arange(wide, dtype=jnp.int32) - REG_ITERS
    inside = ((plane_global >= 0) & (plane_global < nz))[:, None, None]
    gridded = jnp.where(inside, gridded, 0.0)
    iterate = gridded
    for sweep in range(REG_ITERS):
        centre = iterate[1:-1]
        target = gridded[sweep + 1:wide - sweep - 1]
        iterate = centre - 0.25 * (
            centre - target + (2.0 * centre - iterate[:-2] - iterate[2:])
        )
        iterate = jnp.where(inside[sweep + 1:wide - sweep - 1], iterate, 0.0)
    return (iterate[:, :, :cols], iterate[:, :, cols:])


def solution(mesh):
    placed = (P("slab", "ang", None), P("slab", None), P("slab", None), P("slab", None))
    return jax.shard_map(
        on_device,
        mesh=mesh,
        in_specs=placed,
        out_specs=(P("slab", None, "ang"), P("slab", None, "ang")),
        check_vma=False,
    )
```

```python
import math

import jax
import jax.numpy as jnp
from jax import lax
from jax.sharding import PartitionSpec as P

KY = 8
NZ = 1024
REG_ITERS = 2
SPREAD_LOW = 2
SPREAD_HIGH = 3
HALO = SPREAD_LOW + SPREAD_HIGH
CHUNKS = 4


def phase_parts(rows, cols, length):
    row_index = jnp.arange(rows, dtype=jnp.int32)[:, None]
    column = cols[None, :]
    phase_angle = (row_index * column % length).astype(jnp.float32) * (2.0 * math.pi / length)
    return jnp.cos(phase_angle), jnp.sin(phase_angle)


def dft_block(rows, col_hi, length):
    split = 1 << (int(math.log2(length)) // 2)
    cos_hi, sin_hi = phase_parts(rows, col_hi * split, length)
    cos_lo, sin_lo = phase_parts(rows, jnp.arange(split, dtype=jnp.int32), length)
    a, b = cos_hi[:, :, None, None], sin_hi[:, :, None, None]
    c, d = cos_lo[:, None, None, :], sin_lo[:, None, None, :]
    is_re = (jnp.arange(2, dtype=jnp.int32) == 0).reshape(1, 1, 2, 1)
    return jnp.where(is_re, a * c - b * d, -(b * c + a * d)), split


def on_device(projections, dest_plane, sub_offset, ky_bin):
    count_ang = lax.axis_size("ang")
    count_slab = lax.axis_size("slab")
    local_count, quarter, full_width = projections.shape
    height = quarter * count_ang
    cols = full_width // count_ang
    total_cols = 2 * cols
    nz = NZ
    z_dev = nz // count_slab
    per_proj = 2 * z_dev
    me_ang = lax.axis_index("ang")

    edges = jnp.arange(count_slab + 1, dtype=jnp.int32) * z_dev
    start = jnp.sum((dest_plane[:, None, :] < edges[None, :, None]).astype(jnp.int32), axis=2)
    counts = start[:, 1:] - start[:, :-1]
    slot = jnp.arange(per_proj, dtype=jnp.int32)
    valid = slot[None, None, :] < counts[:, :, None]
    row_q = (start[:, :-1, None] + slot[None, None, :] + height // 2) % height
    q_iota = jnp.arange(height, dtype=jnp.int32)
    select = ((row_q[..., None] == q_iota) & valid[..., None]).astype(jnp.bfloat16)
    label_cols = jnp.stack(
        [dest_plane % z_dev, sub_offset, ky_bin, jnp.ones_like(ky_bin)], axis=-1
    ).astype(jnp.bfloat16)
    labels = jnp.einsum("pbjq,pqk->bpjk", select, label_cols, preferred_element_type=jnp.float32)
    arrived_labels = lax.all_to_all(labels, "slab", split_axis=0, concat_axis=0, tiled=True)

    split_w = 1 << (int(math.log2(full_width)) // 2)
    per_block = cols // split_w
    col_hi = ((jnp.arange(count_ang, dtype=jnp.int32)[:, None] + me_ang) % count_ang) * per_block
    col_hi = (col_hi + jnp.arange(per_block, dtype=jnp.int32)[None, :]).reshape(-1)
    table, _ = dft_block(full_width, col_hi, full_width)
    table = table.reshape(full_width, count_ang, per_block, 2, split_w)
    table = jnp.transpose(table, (0, 1, 3, 2, 4)).astype(jnp.bfloat16)
    table = table.reshape(full_width, count_ang, total_cols)

    split_h = 1 << (int(math.log2(height)) // 2)
    h_rot = (me_ang - jnp.arange(count_ang, dtype=jnp.int32)[:, None]) % count_ang * quarter
    h_rot = (h_rot + jnp.arange(quarter, dtype=jnp.int32)[None, :]).reshape(-1)
    q_hi = jnp.arange(height // split_h, dtype=jnp.int32) * split_h
    q_lo = jnp.arange(split_h, dtype=jnp.int32)
    angle_hi = (h_rot[:, None] * q_hi[None, :] % height).astype(jnp.float32) * (2.0 * math.pi / height)
    angle_lo = (h_rot[:, None] * q_lo[None, :] % height).astype(jnp.float32) * (2.0 * math.pi / height)
    a, b = jnp.cos(angle_hi)[None, :, :, None], jnp.sin(angle_hi)[None, :, :, None]
    c, d = jnp.cos(angle_lo)[None, :, None, :], jnp.sin(angle_lo)[None, :, None, :]
    is_cos = (jnp.arange(2, dtype=jnp.int32) == 0).reshape(2, 1, 1, 1)
    lhs_t = jnp.where(is_cos, a * c - b * d, b * c + a * d).astype(jnp.bfloat16)
    lhs_t = lhs_t.reshape(2 * height, height)
    unitary = 1.0 / math.sqrt(height * full_width)

    arrived_rows = []
    held = None
    for p in range(local_count):
        blocks = [
            jnp.dot(projections[p], table[:, shift], preferred_element_type=jnp.float32).astype(jnp.bfloat16)
            for shift in range(count_ang)
        ]
        if held is not None:
            blocks, held = lax.optimization_barrier((blocks, held))
        received = [blocks[0]]
        for shift in range(1, count_ang):
            pairs = [(i, (i + shift) % count_ang) for i in range(count_ang)]
            received.append(lax.ppermute(blocks[shift], "ang", pairs))
        held = received
        direct = jnp.concatenate(received, axis=0)
        swapped = jnp.concatenate([direct[:, cols:], -direct[:, :cols]], axis=1)
        rhs = jnp.concatenate([direct, swapped], axis=0)
        spectrum = lax.dot_general(
            lhs_t, rhs, (((0,), (0,)), ((), ())), preferred_element_type=jnp.float32
        )
        spectrum = (spectrum * unitary).astype(jnp.bfloat16)
        packed = jnp.dot(
            select[p].reshape(count_slab * per_proj, height), spectrum, preferred_element_type=jnp.bfloat16
        )
        arrived_rows.append(
            lax.all_to_all(
                packed.reshape(count_slab, per_proj, total_cols), "slab", split_axis=0, concat_axis=0, tiled=True
            ).reshape(-1, total_cols)
        )

    density = 1.0 / math.sqrt(local_count * count_slab)
    slots = z_dev + HALO + 1
    dest_index = jnp.arange(slots * KY, dtype=jnp.int32)[:, None]
    padded = jnp.zeros((slots * KY, total_cols), jnp.float32)
    for p in range(local_count):
        tags = arrived_labels[:, p].reshape(-1, 4)
        arrived_plane = tags[:, 0].astype(jnp.int32)
        arrived_eighth = tags[:, 1].astype(jnp.int32)
        arrived_ky = tags[:, 2].astype(jnp.int32)
        tag_ok = tags[:, 3] > 0.5
        weights = jnp.zeros((slots * KY, tags.shape[0]), jnp.bfloat16)
        for shift in range(-SPREAD_LOW, SPREAD_HIGH + 1):
            distance = shift - arrived_eighth.astype(jnp.float32) * 0.125
            weight = (jnp.exp(-0.5 * distance * distance) * density).astype(jnp.bfloat16)
            index = (arrived_plane + (shift + SPREAD_HIGH)) * KY + arrived_ky
            hit = (dest_index == index[None, :]) & tag_ok[None, :]
            weights = jnp.where(hit, weight[None, :], weights)
        padded = padded + jnp.dot(weights, arrived_rows[p], preferred_element_type=jnp.float32)
    padded = padded.reshape(slots, KY, total_cols)

    me = lax.axis_index("slab")
    forward = [(i, i + 1) for i in range(count_slab - 1)]
    backward = [(i + 1, i) for i in range(count_slab - 1)]
    from_lower = lax.ppermute(padded[slots - HALO:], "slab", forward)
    from_upper = lax.ppermute(padded[:HALO], "slab", backward)
    window = padded[1:slots - 1]
    wide = z_dev + 2 * REG_ITERS
    gridded = window.at[:HALO].add(from_lower).at[wide - HALO:].add(from_upper)
    plane_global = me * z_dev + jnp.arange(wide, dtype=jnp.int32) - REG_ITERS
    inside = ((plane_global >= 0) & (plane_global < nz))[:, None, None]
    gridded = jnp.where(inside, gridded, 0.0)
    iterate = gridded
    for sweep in range(REG_ITERS):
        centre = iterate[1:-1]
        target = gridded[sweep + 1:wide - sweep - 1]
        iterate = centre - 0.25 * (
            centre - target + (2.0 * centre - iterate[:-2] - iterate[2:])
        )
        iterate = jnp.where(inside[sweep + 1:wide - sweep - 1], iterate, 0.0)
    return (iterate[:, :, :cols], iterate[:, :, cols:])


def solution(mesh):
    placed = (P("slab", "ang", None), P("slab", None), P("slab", None), P("slab", None))
    return jax.shard_map(
        on_device,
        mesh=mesh,
        in_specs=placed,
        out_specs=(P("slab", None, "ang"), P("slab", None, "ang")),
        check_vma=False,
    )
```

```python
import math

import jax
import jax.numpy as jnp
from jax import lax
from jax.sharding import PartitionSpec as P

KY = 8
NZ = 1024
REG_ITERS = 2
SPREAD_LOW = 2
SPREAD_HIGH = 3
HALO = SPREAD_LOW + SPREAD_HIGH
CHUNKS = 4


def phase_parts(rows, cols, length):
    row_index = jnp.arange(rows, dtype=jnp.int32)[:, None]
    column = cols[None, :]
    phase_angle = (row_index * column % length).astype(jnp.float32) * (2.0 * math.pi / length)
    return jnp.cos(phase_angle), jnp.sin(phase_angle)


def dft_block(rows, col_hi, length):
    split = 1 << (int(math.log2(length)) // 2)
    cos_hi, sin_hi = phase_parts(rows, col_hi * split, length)
    cos_lo, sin_lo = phase_parts(rows, jnp.arange(split, dtype=jnp.int32), length)
    a, b = cos_hi[:, :, None, None], sin_hi[:, :, None, None]
    c, d = cos_lo[:, None, None, :], sin_lo[:, None, None, :]
    is_re = (jnp.arange(2, dtype=jnp.int32) == 0).reshape(1, 1, 2, 1)
    return jnp.where(is_re, a * c - b * d, -(b * c + a * d)), split


def on_device(projections, dest_plane, sub_offset, ky_bin):
    count_ang = lax.axis_size("ang")
    count_slab = lax.axis_size("slab")
    local_count, quarter, full_width = projections.shape
    height = quarter * count_ang
    cols = full_width // count_ang
    total_cols = 2 * cols
    nz = NZ
    z_dev = nz // count_slab
    per_proj = 2 * z_dev
    me_ang = lax.axis_index("ang")

    edges = jnp.arange(count_slab + 1, dtype=jnp.int32) * z_dev
    start = jnp.sum((dest_plane[:, None, :] < edges[None, :, None]).astype(jnp.int32), axis=2)
    counts = start[:, 1:] - start[:, :-1]
    slot = jnp.arange(per_proj, dtype=jnp.int32)
    valid = slot[None, None, :] < counts[:, :, None]
    row_q = (start[:, :-1, None] + slot[None, None, :] + height // 2) % height
    q_iota = jnp.arange(height, dtype=jnp.int32)
    select = ((row_q[..., None] == q_iota) & valid[..., None]).astype(jnp.bfloat16)
    label_cols = jnp.stack(
        [dest_plane % z_dev, sub_offset, ky_bin, jnp.ones_like(ky_bin)], axis=-1
    ).astype(jnp.bfloat16)
    labels = jnp.einsum("pbjq,pqk->bpjk", select, label_cols, preferred_element_type=jnp.float32)
    arrived_labels = lax.all_to_all(labels, "slab", split_axis=0, concat_axis=0, tiled=True)

    split_w = 1 << (int(math.log2(full_width)) // 2)
    per_block = cols // split_w
    col_hi = ((jnp.arange(count_ang, dtype=jnp.int32)[:, None] + me_ang) % count_ang) * per_block
    col_hi = (col_hi + jnp.arange(per_block, dtype=jnp.int32)[None, :]).reshape(-1)
    table, _ = dft_block(full_width, col_hi, full_width)
    table = table.reshape(full_width, count_ang, per_block, 2, split_w)
    table = jnp.transpose(table, (0, 1, 3, 2, 4)).astype(jnp.bfloat16)
    table = table.reshape(full_width, count_ang, total_cols)

    split_h = 1 << (int(math.log2(height)) // 2)
    per_quarter = quarter // split_h
    h_hi = ((me_ang - jnp.arange(count_ang, dtype=jnp.int32)[:, None]) % count_ang) * per_quarter
    h_hi = (h_hi + jnp.arange(per_quarter, dtype=jnp.int32)[None, :]).reshape(-1) * split_h
    h_lo = jnp.arange(split_h, dtype=jnp.int32)
    slot_q = row_q.reshape(local_count, -1)
    slot_ok = valid.reshape(local_count, -1)
    step = 2.0 * math.pi / height
    angle_hi = (slot_q[:, :, None] * h_hi[None, None, :] % height).astype(jnp.float32) * step
    angle_lo = (slot_q[:, :, None] * h_lo[None, None, :] % height).astype(jnp.float32) * step
    ca, sa = jnp.cos(angle_hi)[:, :, None, :, None], jnp.sin(angle_hi)[:, :, None, :, None]
    cb, sb = jnp.cos(angle_lo)[:, :, None, None, :], jnp.sin(angle_lo)[:, :, None, None, :]
    is_cos = (jnp.arange(2, dtype=jnp.int32) == 0).reshape(1, 1, 2, 1, 1)
    picked = jnp.where(is_cos, ca * cb - sa * sb, sa * cb + ca * sb)
    picked = jnp.where(slot_ok[:, :, None, None, None], picked, 0.0).astype(jnp.bfloat16)
    picked = picked.reshape(local_count, count_slab * per_proj, 2 * height)
    unitary = 1.0 / math.sqrt(height * full_width)

    arrived_rows = []
    held = None
    for p in range(local_count):
        blocks = [
            jnp.dot(projections[p], table[:, shift], preferred_element_type=jnp.float32).astype(jnp.bfloat16)
            for shift in range(count_ang)
        ]
        if held is not None:
            blocks, held = lax.optimization_barrier((blocks, held))
        received = [blocks[0]]
        for shift in range(1, count_ang):
            pairs = [(i, (i + shift) % count_ang) for i in range(count_ang)]
            received.append(lax.ppermute(blocks[shift], "ang", pairs))
        held = received
        direct = jnp.concatenate(received, axis=0)
        swapped = jnp.concatenate([direct[:, cols:], -direct[:, :cols]], axis=1)
        rhs = jnp.concatenate([direct, swapped], axis=0)
        packed = jnp.dot(picked[p], rhs, preferred_element_type=jnp.float32)
        packed = (packed * unitary).astype(jnp.bfloat16)
        arrived_rows.append(
            lax.all_to_all(
                packed.reshape(count_slab, per_proj, total_cols), "slab", split_axis=0, concat_axis=0, tiled=True
            ).reshape(-1, total_cols)
        )

    density = 1.0 / math.sqrt(local_count * count_slab)
    slots = z_dev + HALO + 1
    dest_index = jnp.arange(slots * KY, dtype=jnp.int32)[:, None]
    padded = jnp.zeros((slots * KY, total_cols), jnp.float32)
    for p in range(local_count):
        tags = arrived_labels[:, p].reshape(-1, 4)
        arrived_plane = tags[:, 0].astype(jnp.int32)
        arrived_eighth = tags[:, 1].astype(jnp.int32)
        arrived_ky = tags[:, 2].astype(jnp.int32)
        tag_ok = tags[:, 3] > 0.5
        weights = jnp.zeros((slots * KY, tags.shape[0]), jnp.bfloat16)
        for shift in range(-SPREAD_LOW, SPREAD_HIGH + 1):
            distance = shift - arrived_eighth.astype(jnp.float32) * 0.125
            weight = (jnp.exp(-0.5 * distance * distance) * density).astype(jnp.bfloat16)
            index = (arrived_plane + (shift + SPREAD_HIGH)) * KY + arrived_ky
            hit = (dest_index == index[None, :]) & tag_ok[None, :]
            weights = jnp.where(hit, weight[None, :], weights)
        padded = padded + jnp.dot(weights, arrived_rows[p], preferred_element_type=jnp.float32)
    padded = padded.reshape(slots, KY, total_cols)

    me = lax.axis_index("slab")
    forward = [(i, i + 1) for i in range(count_slab - 1)]
    backward = [(i + 1, i) for i in range(count_slab - 1)]
    from_lower = lax.ppermute(padded[slots - HALO:], "slab", forward)
    from_upper = lax.ppermute(padded[:HALO], "slab", backward)
    window = padded[1:slots - 1]
    wide = z_dev + 2 * REG_ITERS
    gridded = window.at[:HALO].add(from_lower).at[wide - HALO:].add(from_upper)
    plane_global = me * z_dev + jnp.arange(wide, dtype=jnp.int32) - REG_ITERS
    inside = ((plane_global >= 0) & (plane_global < nz))[:, None, None]
    gridded = jnp.where(inside, gridded, 0.0)
    iterate = gridded
    for sweep in range(REG_ITERS):
        centre = iterate[1:-1]
        target = gridded[sweep + 1:wide - sweep - 1]
        iterate = centre - 0.25 * (
            centre - target + (2.0 * centre - iterate[:-2] - iterate[2:])
        )
        iterate = jnp.where(inside[sweep + 1:wide - sweep - 1], iterate, 0.0)
    return (iterate[:, :, :cols], iterate[:, :, cols:])


def solution(mesh):
    placed = (P("slab", "ang", None), P("slab", None), P("slab", None), P("slab", None))
    return jax.shard_map(
        on_device,
        mesh=mesh,
        in_specs=placed,
        out_specs=(P("slab", None, "ang"), P("slab", None, "ang")),
        check_vma=False,
    )
```

```python
import math

import jax
import jax.numpy as jnp
from jax import lax
from jax.sharding import PartitionSpec as P


KY = 8
NZ = 1024
REG_ITERS = 2
SPREAD_LOW = 2
SPREAD_HIGH = 3
HALO = SPREAD_LOW + SPREAD_HIGH


def phase_parts(rows, cols, length):
    row_index = jnp.arange(rows, dtype=jnp.int32)[:, None]
    column = cols[None, :]
    phase_angle = (row_index * column % length).astype(jnp.float32) * (2.0 * math.pi / length)
    return jnp.cos(phase_angle), jnp.sin(phase_angle)


def dft_block(rows, col_hi, length):
    split = 1 << (int(math.log2(length)) // 2)
    cos_hi, sin_hi = phase_parts(rows, col_hi * split, length)
    cos_lo, sin_lo = phase_parts(rows, jnp.arange(split, dtype=jnp.int32), length)
    a, b = cos_hi[:, :, None, None], sin_hi[:, :, None, None]
    c, d = cos_lo[:, None, None, :], sin_lo[:, None, None, :]
    is_re = (jnp.arange(2, dtype=jnp.int32) == 0).reshape(1, 1, 2, 1)
    return jnp.where(is_re, a * c - b * d, -(b * c + a * d)), split


def on_device(projections, dest_plane, sub_offset, ky_bin):
    count_ang = lax.axis_size("ang")
    count_slab = lax.axis_size("slab")
    local_count, quarter, full_width = projections.shape
    height = quarter * count_ang
    cols = full_width // count_ang
    total_cols = 2 * cols
    nz = NZ
    z_dev = nz // count_slab
    per_proj = 2 * z_dev
    me_ang = lax.axis_index("ang")

    edges = jnp.arange(count_slab + 1, dtype=jnp.int32) * z_dev
    start = jnp.sum((dest_plane[:, None, :] < edges[None, :, None]).astype(jnp.int32), axis=2)
    counts = start[:, 1:] - start[:, :-1]
    slot = jnp.arange(per_proj, dtype=jnp.int32)
    valid = slot[None, None, :] < counts[:, :, None]
    row_q = (start[:, :-1, None] + slot[None, None, :] + height // 2) % height
    q_iota = jnp.arange(height, dtype=jnp.int32)
    select = ((row_q[..., None] == q_iota) & valid[..., None]).astype(jnp.bfloat16)
    label_cols = jnp.stack(
        [dest_plane % z_dev, sub_offset, ky_bin, jnp.ones_like(ky_bin)], axis=-1
    ).astype(jnp.bfloat16)
    labels = jnp.einsum("pbjq,pqk->bpjk", select, label_cols, preferred_element_type=jnp.float32)
    arrived_labels = lax.all_to_all(labels, "slab", split_axis=0, concat_axis=0, tiled=True)

    split_w = 1 << (int(math.log2(full_width)) // 2)
    per_block = cols // split_w
    col_hi = ((jnp.arange(count_ang, dtype=jnp.int32)[:, None] + me_ang) % count_ang) * per_block
    col_hi = (col_hi + jnp.arange(per_block, dtype=jnp.int32)[None, :]).reshape(-1)
    table, _ = dft_block(full_width, col_hi, full_width)
    table = table.reshape(full_width, count_ang, per_block, 2, split_w)
    table = jnp.transpose(table, (0, 1, 3, 2, 4)).astype(jnp.bfloat16)
    table = table.reshape(full_width, count_ang, total_cols)

    split_h = 1 << (int(math.log2(height)) // 2)
    per_quarter = quarter // split_h
    h_hi = ((me_ang - jnp.arange(count_ang, dtype=jnp.int32)[:, None]) % count_ang) * per_quarter
    h_hi = (h_hi + jnp.arange(per_quarter, dtype=jnp.int32)[None, :]).reshape(-1) * split_h
    h_lo = jnp.arange(split_h, dtype=jnp.int32)
    slot_q = row_q.reshape(local_count, -1)
    slot_ok = valid.reshape(local_count, -1)
    step = 2.0 * math.pi / height
    angle_hi = (slot_q[:, :, None] * h_hi[None, None, :] % height).astype(jnp.float32) * step
    angle_lo = (slot_q[:, :, None] * h_lo[None, None, :] % height).astype(jnp.float32) * step
    ca, sa = jnp.cos(angle_hi)[:, :, None, :, None], jnp.sin(angle_hi)[:, :, None, :, None]
    cb, sb = jnp.cos(angle_lo)[:, :, None, None, :], jnp.sin(angle_lo)[:, :, None, None, :]
    is_cos = (jnp.arange(2, dtype=jnp.int32) == 0).reshape(1, 1, 2, 1, 1)
    picked = jnp.where(is_cos, ca * cb - sa * sb, sa * cb + ca * sb)
    picked = jnp.where(slot_ok[:, :, None, None, None], picked, 0.0).astype(jnp.bfloat16)
    picked = picked.reshape(local_count, count_slab * per_proj, 2 * height)
    unitary = 1.0 / math.sqrt(height * full_width)

    arrived_rows = []
    held = None
    for p in range(local_count):
        blocks = [
            jnp.dot(projections[p], table[:, shift], preferred_element_type=jnp.float32).astype(
                jnp.bfloat16
            )
            for shift in range(count_ang)
        ]
        if held is not None:
            blocks, held = lax.optimization_barrier((blocks, held))
        received = [blocks[0]]
        for shift in range(1, count_ang):
            pairs = [(i, (i + shift) % count_ang) for i in range(count_ang)]
            received.append(lax.ppermute(blocks[shift], "ang", pairs))
        held = received
        direct = jnp.concatenate(received, axis=0)
        swapped = jnp.concatenate([direct[:, cols:], -direct[:, :cols]], axis=1)
        rhs = jnp.concatenate([direct, swapped], axis=0)
        packed = jnp.dot(picked[p], rhs, preferred_element_type=jnp.float32)
        packed = (packed * unitary).astype(jnp.bfloat16)
        arrived_rows.append(
            lax.all_to_all(
                packed.reshape(count_slab, per_proj, total_cols), "slab", split_axis=0, concat_axis=0,
                tiled=True,
            ).reshape(-1, total_cols)
        )

    density = 1.0 / math.sqrt(local_count * count_slab)
    slots = z_dev + HALO + 1
    dest_index = jnp.arange(slots * KY, dtype=jnp.int32)[:, None]
    padded = jnp.zeros((slots * KY, total_cols), jnp.float32)
    for p in range(local_count):
        tags = arrived_labels[:, p].reshape(-1, 4)
        arrived_plane = tags[:, 0].astype(jnp.int32)
        arrived_eighth = tags[:, 1].astype(jnp.int32)
        arrived_ky = tags[:, 2].astype(jnp.int32)
        tag_ok = tags[:, 3] > 0.5
        weights = jnp.zeros((slots * KY, tags.shape[0]), jnp.bfloat16)
        for shift in range(-SPREAD_LOW, SPREAD_HIGH + 1):
            distance = shift - arrived_eighth.astype(jnp.float32) * 0.125
            weight = (jnp.exp(-0.5 * distance * distance) * density).astype(jnp.bfloat16)
            index = (arrived_plane + (shift + SPREAD_HIGH)) * KY + arrived_ky
            hit = (dest_index == index[None, :]) & tag_ok[None, :]
            weights = jnp.where(hit, weight[None, :], weights)
        weights = lax.optimization_barrier(weights)
        padded = padded + jnp.dot(weights, arrived_rows[p], preferred_element_type=jnp.float32)
    padded = padded.reshape(slots, KY, total_cols)

    me = lax.axis_index("slab")
    forward = [(i, i + 1) for i in range(count_slab - 1)]
    backward = [(i + 1, i) for i in range(count_slab - 1)]
    from_lower = lax.ppermute(padded[slots - HALO:], "slab", forward)
    from_upper = lax.ppermute(padded[:HALO], "slab", backward)
    window = padded[1:slots - 1]
    wide = z_dev + 2 * REG_ITERS
    gridded = window.at[:HALO].add(from_lower).at[wide - HALO:].add(from_upper)
    plane_global = me * z_dev + jnp.arange(wide, dtype=jnp.int32) - REG_ITERS
    inside = ((plane_global >= 0) & (plane_global < nz))[:, None, None]
    gridded = jnp.where(inside, gridded, 0.0)
    iterate = gridded
    for sweep in range(REG_ITERS):
        centre = iterate[1:-1]
        target = gridded[sweep + 1:wide - sweep - 1]
        iterate = centre - 0.25 * (
            centre - target + (2.0 * centre - iterate[:-2] - iterate[2:])
        )
        iterate = jnp.where(inside[sweep + 1:wide - sweep - 1], iterate, 0.0)
    return (iterate[:, :, :cols], iterate[:, :, cols:])


def solution(mesh):
    placed = (P("slab", "ang", None), P("slab", None), P("slab", None), P("slab", None))
    return jax.shard_map(
        on_device,
        mesh=mesh,
        in_specs=placed,
        out_specs=(P("slab", None, "ang"), P("slab", None, "ang")),
        check_vma=False,
    )
```

```python
import math

import jax
import jax.numpy as jnp
from jax import lax
from jax.sharding import PartitionSpec as P


KY = 8
NZ = 1024
REG_ITERS = 2
SPREAD_LOW = 2
SPREAD_HIGH = 3
HALO = SPREAD_LOW + SPREAD_HIGH


def phase_parts(rows, cols, length):
    row_index = jnp.arange(rows, dtype=jnp.int32)[:, None]
    column = cols[None, :]
    phase_angle = (row_index * column % length).astype(jnp.float32) * (2.0 * math.pi / length)
    return jnp.cos(phase_angle), jnp.sin(phase_angle)


def dft_block(rows, col_hi, length):
    split = 1 << (int(math.log2(length)) // 2)
    cos_hi, sin_hi = phase_parts(rows, col_hi * split, length)
    cos_lo, sin_lo = phase_parts(rows, jnp.arange(split, dtype=jnp.int32), length)
    a, b = cos_hi[:, :, None, None], sin_hi[:, :, None, None]
    c, d = cos_lo[:, None, None, :], sin_lo[:, None, None, :]
    is_re = (jnp.arange(2, dtype=jnp.int32) == 0).reshape(1, 1, 2, 1)
    return jnp.where(is_re, a * c - b * d, -(b * c + a * d)), split


def on_device(projections, dest_plane, sub_offset, ky_bin):
    count_ang = lax.axis_size("ang")
    count_slab = lax.axis_size("slab")
    local_count, quarter, full_width = projections.shape
    height = quarter * count_ang
    cols = full_width // count_ang
    total_cols = 2 * cols
    nz = NZ
    z_dev = nz // count_slab
    per_proj = 2 * z_dev
    me_ang = lax.axis_index("ang")

    edges = jnp.arange(count_slab + 1, dtype=jnp.int32) * z_dev
    start = jnp.sum((dest_plane[:, None, :] < edges[None, :, None]).astype(jnp.int32), axis=2)
    counts = start[:, 1:] - start[:, :-1]
    slot = jnp.arange(per_proj, dtype=jnp.int32)
    valid = slot[None, None, :] < counts[:, :, None]
    row_q = (start[:, :-1, None] + slot[None, None, :] + height // 2) % height
    q_iota = jnp.arange(height, dtype=jnp.int32)
    select = ((row_q[..., None] == q_iota) & valid[..., None]).astype(jnp.bfloat16)
    label_cols = jnp.stack(
        [dest_plane % z_dev, sub_offset, ky_bin, jnp.ones_like(ky_bin)], axis=-1
    ).astype(jnp.bfloat16)
    labels = jnp.einsum("pbjq,pqk->bpjk", select, label_cols, preferred_element_type=jnp.float32)
    arrived_labels = lax.all_to_all(labels, "slab", split_axis=0, concat_axis=0, tiled=True)

    split_w = 1 << (int(math.log2(full_width)) // 2)
    per_block = cols // split_w
    col_hi = ((jnp.arange(count_ang, dtype=jnp.int32)[:, None] + me_ang) % count_ang) * per_block
    col_hi = (col_hi + jnp.arange(per_block, dtype=jnp.int32)[None, :]).reshape(-1)
    table, _ = dft_block(full_width, col_hi, full_width)
    table = table.reshape(full_width, count_ang, per_block, 2, split_w)
    table = jnp.transpose(table, (0, 1, 3, 2, 4)).astype(jnp.bfloat16)
    table = table.reshape(full_width, count_ang, total_cols)

    split_h = 1 << (int(math.log2(height)) // 2)
    per_quarter = quarter // split_h
    h_hi = ((me_ang - jnp.arange(count_ang, dtype=jnp.int32)[:, None]) % count_ang) * per_quarter
    h_hi = (h_hi + jnp.arange(per_quarter, dtype=jnp.int32)[None, :]).reshape(-1) * split_h
    h_lo = jnp.arange(split_h, dtype=jnp.int32)
    slot_q = row_q.reshape(local_count, -1)
    slot_ok = valid.reshape(local_count, -1)
    step = 2.0 * math.pi / height

    def picked_t(p):
        angle_hi = (h_hi[:, None] * slot_q[p][None, :] % height).astype(jnp.float32) * step
        angle_lo = (h_lo[:, None] * slot_q[p][None, :] % height).astype(jnp.float32) * step
        ca, sa = jnp.cos(angle_hi)[None, :, None, :], jnp.sin(angle_hi)[None, :, None, :]
        cb, sb = jnp.cos(angle_lo)[None, None, :, :], jnp.sin(angle_lo)[None, None, :, :]
        is_cos = (jnp.arange(2, dtype=jnp.int32) == 0).reshape(2, 1, 1, 1)
        rows = jnp.where(is_cos, ca * cb - sa * sb, sa * cb + ca * sb)
        rows = jnp.where(slot_ok[p][None, None, None, :], rows, 0.0).astype(jnp.bfloat16)
        return rows.reshape(2 * height, count_slab * per_proj)

    def picked_rows(p):
        angle_hi = (slot_q[p][:, None] * h_hi[None, :] % height).astype(jnp.float32) * step
        angle_lo = (slot_q[p][:, None] * h_lo[None, :] % height).astype(jnp.float32) * step
        ca, sa = jnp.cos(angle_hi)[:, None, :, None], jnp.sin(angle_hi)[:, None, :, None]
        cb, sb = jnp.cos(angle_lo)[:, None, None, :], jnp.sin(angle_lo)[:, None, None, :]
        is_cos = (jnp.arange(2, dtype=jnp.int32) == 0).reshape(1, 2, 1, 1)
        rows = jnp.where(is_cos, ca * cb - sa * sb, sa * cb + ca * sb)
        rows = jnp.where(slot_ok[p][:, None, None, None], rows, 0.0).astype(jnp.bfloat16)
        return rows.reshape(count_slab * per_proj, 2 * height)

    unitary = 1.0 / math.sqrt(height * full_width)

    arrived_rows = []
    held = None
    for p in range(local_count):
        transformed = jnp.dot(
            projections[p], table.reshape(full_width, count_ang * total_cols),
            preferred_element_type=jnp.float32,
        ).astype(jnp.bfloat16)
        blocks = [transformed[:, shift * total_cols:(shift + 1) * total_cols] for shift in range(count_ang)]
        if held is not None:
            blocks, held = lax.optimization_barrier((blocks, held))
        received = [blocks[0]]
        for shift in range(1, count_ang):
            pairs = [(i, (i + shift) % count_ang) for i in range(count_ang)]
            received.append(lax.ppermute(blocks[shift], "ang", pairs))
        held = received
        direct = jnp.concatenate(received, axis=0)
        swapped = jnp.concatenate([direct[:, cols:], -direct[:, :cols]], axis=1)
        rhs = jnp.concatenate([direct, swapped], axis=0)
        if p == 0:
            packed = jnp.dot(picked_rows(0), rhs, preferred_element_type=jnp.float32)
        else:
            packed = lax.dot_general(
                picked_t(p), rhs, (((0,), (0,)), ((), ())), preferred_element_type=jnp.float32
            )
        packed = (packed * unitary).astype(jnp.bfloat16)
        arrived_rows.append(
            lax.all_to_all(
                packed.reshape(count_slab, per_proj, total_cols), "slab", split_axis=0, concat_axis=0,
                tiled=True,
            ).reshape(-1, total_cols)
        )

    density = 1.0 / math.sqrt(local_count * count_slab)
    slots = z_dev + HALO + 1
    dest_index = jnp.arange(slots * KY, dtype=jnp.int32)[:, None]
    padded = jnp.zeros((slots * KY, total_cols), jnp.float32)
    for p in range(local_count):
        tags = arrived_labels[:, p].reshape(-1, 4)
        arrived_plane = tags[:, 0].astype(jnp.int32)
        arrived_eighth = tags[:, 1].astype(jnp.int32)
        arrived_ky = tags[:, 2].astype(jnp.int32)
        tag_ok = tags[:, 3] > 0.5
        weights = jnp.zeros((slots * KY, tags.shape[0]), jnp.bfloat16)
        for shift in range(-SPREAD_LOW, SPREAD_HIGH + 1):
            distance = shift - arrived_eighth.astype(jnp.float32) * 0.125
            weight = (jnp.exp(-0.5 * distance * distance) * density).astype(jnp.bfloat16)
            index = (arrived_plane + (shift + SPREAD_HIGH)) * KY + arrived_ky
            hit = (dest_index == index[None, :]) & tag_ok[None, :]
            weights = jnp.where(hit, weight[None, :], weights)
        padded = padded + jnp.dot(weights, arrived_rows[p], preferred_element_type=jnp.float32)
    padded = padded.reshape(slots, KY, total_cols)

    me = lax.axis_index("slab")
    forward = [(i, i + 1) for i in range(count_slab - 1)]
    backward = [(i + 1, i) for i in range(count_slab - 1)]
    from_lower = lax.ppermute(padded[slots - HALO:], "slab", forward)
    from_upper = lax.ppermute(padded[:HALO], "slab", backward)
    window = padded[1:slots - 1]
    wide = z_dev + 2 * REG_ITERS
    gridded = window.at[:HALO].add(from_lower).at[wide - HALO:].add(from_upper)
    plane_global = me * z_dev + jnp.arange(wide, dtype=jnp.int32) - REG_ITERS
    inside = ((plane_global >= 0) & (plane_global < nz))[:, None, None]
    gridded = jnp.where(inside, gridded, 0.0)
    iterate = gridded
    for sweep in range(REG_ITERS):
        centre = iterate[1:-1]
        target = gridded[sweep + 1:wide - sweep - 1]
        iterate = centre - 0.25 * (
            centre - target + (2.0 * centre - iterate[:-2] - iterate[2:])
        )
        iterate = jnp.where(inside[sweep + 1:wide - sweep - 1], iterate, 0.0)
    return (iterate[:, :, :cols], iterate[:, :, cols:])


def solution(mesh):
    placed = (P("slab", "ang", None), P("slab", None), P("slab", None), P("slab", None))
    return jax.shard_map(
        on_device,
        mesh=mesh,
        in_specs=placed,
        out_specs=(P("slab", None, "ang"), P("slab", None, "ang")),
        check_vma=False,
    )
```

```python
import math

import jax
import jax.numpy as jnp
from jax import lax
from jax.sharding import PartitionSpec as P


KY = 8
NZ = 1024
REG_ITERS = 2
SPREAD_LOW = 2
SPREAD_HIGH = 3
HALO = SPREAD_LOW + SPREAD_HIGH


def phase_parts(rows, cols, length):
    row_index = jnp.arange(rows, dtype=jnp.int32)[:, None]
    column = cols[None, :]
    phase_angle = (row_index * column % length).astype(jnp.float32) * (2.0 * math.pi / length)
    return jnp.cos(phase_angle), jnp.sin(phase_angle)


def dft_block(rows, col_hi, length):
    split = 1 << (int(math.log2(length)) // 2)
    cos_hi, sin_hi = phase_parts(rows, col_hi * split, length)
    cos_lo, sin_lo = phase_parts(rows, jnp.arange(split, dtype=jnp.int32), length)
    a, b = cos_hi[:, :, None, None], sin_hi[:, :, None, None]
    c, d = cos_lo[:, None, None, :], sin_lo[:, None, None, :]
    is_re = (jnp.arange(2, dtype=jnp.int32) == 0).reshape(1, 1, 2, 1)
    return jnp.where(is_re, a * c - b * d, -(b * c + a * d)), split


def on_device(projections, dest_plane, sub_offset, ky_bin):
    count_ang = lax.axis_size("ang")
    count_slab = lax.axis_size("slab")
    local_count, quarter, full_width = projections.shape
    height = quarter * count_ang
    cols = full_width // count_ang
    total_cols = 2 * cols
    nz = NZ
    z_dev = nz // count_slab
    per_proj = 2 * z_dev
    me_ang = lax.axis_index("ang")

    edges = jnp.arange(count_slab + 1, dtype=jnp.int32) * z_dev
    start = jnp.sum((dest_plane[:, None, :] < edges[None, :, None]).astype(jnp.int32), axis=2)
    counts = start[:, 1:] - start[:, :-1]
    slot = jnp.arange(per_proj, dtype=jnp.int32)
    valid = slot[None, None, :] < counts[:, :, None]
    row_q = (start[:, :-1, None] + slot[None, None, :] + height // 2) % height
    q_iota = jnp.arange(height, dtype=jnp.int32)
    select = ((row_q[..., None] == q_iota) & valid[..., None]).astype(jnp.bfloat16)
    label_cols = jnp.stack(
        [dest_plane % z_dev, sub_offset, ky_bin, jnp.ones_like(ky_bin)], axis=-1
    ).astype(jnp.bfloat16)
    labels = jnp.einsum("pbjq,pqk->bpjk", select, label_cols, preferred_element_type=jnp.float32)
    arrived_labels = lax.all_to_all(labels, "slab", split_axis=0, concat_axis=0, tiled=True)

    split_w = 1 << (int(math.log2(full_width)) // 2)
    per_block = cols // split_w
    col_hi = ((jnp.arange(count_ang, dtype=jnp.int32)[:, None] + me_ang) % count_ang) * per_block
    col_hi = (col_hi + jnp.arange(per_block, dtype=jnp.int32)[None, :]).reshape(-1)
    table, _ = dft_block(full_width, col_hi, full_width)
    table = table.reshape(full_width, count_ang, per_block, 2, split_w)
    table = jnp.transpose(table, (0, 1, 3, 2, 4)).astype(jnp.bfloat16)
    table = table.reshape(full_width, count_ang, total_cols)

    split_h = 1 << (int(math.log2(height)) // 2)
    per_quarter = quarter // split_h
    h_hi = ((me_ang - jnp.arange(count_ang, dtype=jnp.int32)[:, None]) % count_ang) * per_quarter
    h_hi = (h_hi + jnp.arange(per_quarter, dtype=jnp.int32)[None, :]).reshape(-1) * split_h
    h_lo = jnp.arange(split_h, dtype=jnp.int32)
    slot_q = row_q.reshape(local_count, -1)
    slot_ok = valid.reshape(local_count, -1)
    step = 2.0 * math.pi / height
    angle_hi = (slot_q[:, :, None] * h_hi[None, None, :] % height).astype(jnp.float32) * step
    angle_lo = (slot_q[:, :, None] * h_lo[None, None, :] % height).astype(jnp.float32) * step
    ca, sa = jnp.cos(angle_hi)[:, :, None, :, None], jnp.sin(angle_hi)[:, :, None, :, None]
    cb, sb = jnp.cos(angle_lo)[:, :, None, None, :], jnp.sin(angle_lo)[:, :, None, None, :]
    is_cos = (jnp.arange(2, dtype=jnp.int32) == 0).reshape(1, 1, 2, 1, 1)
    picked = jnp.where(is_cos, ca * cb - sa * sb, sa * cb + ca * sb)
    picked = jnp.where(slot_ok[:, :, None, None, None], picked, 0.0).astype(jnp.bfloat16)
    picked = picked.reshape(local_count, count_slab * per_proj, 2 * height)
    unitary = 1.0 / math.sqrt(height * full_width)

    arrived_rows = []
    held = None
    for p in range(local_count):
        transformed = jnp.dot(
            projections[p], table.reshape(full_width, count_ang * total_cols),
            preferred_element_type=jnp.float32,
        ).astype(jnp.bfloat16)
        blocks = [transformed[:, shift * total_cols:(shift + 1) * total_cols] for shift in range(count_ang)]
        if held is not None:
            blocks, held = lax.optimization_barrier((blocks, held))
        received = [blocks[0]]
        for shift in range(1, count_ang):
            pairs = [(i, (i + shift) % count_ang) for i in range(count_ang)]
            received.append(lax.ppermute(blocks[shift], "ang", pairs))
        held = received
        direct = jnp.concatenate(received, axis=0)
        swapped = jnp.concatenate([direct[:, cols:], -direct[:, :cols]], axis=1)
        rhs = jnp.concatenate([direct, swapped], axis=0)
        packed = jnp.dot(picked[p], rhs, preferred_element_type=jnp.float32)
        packed = (packed * unitary).astype(jnp.bfloat16)
        arrived_rows.append(
            lax.all_to_all(
                packed.reshape(count_slab, per_proj, total_cols), "slab", split_axis=0, concat_axis=0,
                tiled=True,
            ).reshape(-1, total_cols)
        )

    density = 1.0 / math.sqrt(local_count * count_slab)
    slots = z_dev + HALO + 1
    dest_index = jnp.arange(slots * KY, dtype=jnp.int32)[:, None]
    padded = jnp.zeros((slots * KY, total_cols), jnp.float32)
    for p in range(local_count):
        tags = arrived_labels[:, p].reshape(-1, 4)
        arrived_plane = tags[:, 0].astype(jnp.int32)
        arrived_eighth = tags[:, 1].astype(jnp.int32)
        arrived_ky = tags[:, 2].astype(jnp.int32)
        tag_ok = tags[:, 3] > 0.5
        weights = jnp.zeros((slots * KY, tags.shape[0]), jnp.bfloat16)
        for shift in range(-SPREAD_LOW, SPREAD_HIGH + 1):
            distance = shift - arrived_eighth.astype(jnp.float32) * 0.125
            weight = (jnp.exp(-0.5 * distance * distance) * density).astype(jnp.bfloat16)
            index = (arrived_plane + (shift + SPREAD_HIGH)) * KY + arrived_ky
            hit = (dest_index == index[None, :]) & tag_ok[None, :]
            weights = jnp.where(hit, weight[None, :], weights)
        weights = lax.optimization_barrier(weights)
        padded = padded + jnp.dot(weights, arrived_rows[p], preferred_element_type=jnp.float32)
    padded = padded.reshape(slots, KY, total_cols)

    me = lax.axis_index("slab")
    forward = [(i, i + 1) for i in range(count_slab - 1)]
    backward = [(i + 1, i) for i in range(count_slab - 1)]
    from_lower = lax.ppermute(padded[slots - HALO:], "slab", forward)
    from_upper = lax.ppermute(padded[:HALO], "slab", backward)
    window = padded[1:slots - 1]
    wide = z_dev + 2 * REG_ITERS
    gridded = window.at[:HALO].add(from_lower).at[wide - HALO:].add(from_upper)
    plane_global = me * z_dev + jnp.arange(wide, dtype=jnp.int32) - REG_ITERS
    inside = ((plane_global >= 0) & (plane_global < nz))[:, None, None]
    gridded = jnp.where(inside, gridded, 0.0)
    iterate = gridded
    for sweep in range(REG_ITERS):
        centre = iterate[1:-1]
        target = gridded[sweep + 1:wide - sweep - 1]
        iterate = centre - 0.25 * (
            centre - target + (2.0 * centre - iterate[:-2] - iterate[2:])
        )
        iterate = jnp.where(inside[sweep + 1:wide - sweep - 1], iterate, 0.0)
    return (iterate[:, :, :cols], iterate[:, :, cols:])


def solution(mesh):
    placed = (P("slab", "ang", None), P("slab", None), P("slab", None), P("slab", None))
    return jax.shard_map(
        on_device,
        mesh=mesh,
        in_specs=placed,
        out_specs=(P("slab", None, "ang"), P("slab", None, "ang")),
        check_vma=False,
    )
```
